128 devices in a mesh: seq: 4 (over x_hi, core), tensor: 32 (over y, x_lo, z).
Axes of the slice: x: 4 (x_hi: 2, x_lo: 2; x = x_hi * 2 + x_lo), y: 4, z: 4, core: 2. Of those that a mesh axis runs over, the one named last changes fastest.
Arguments:
- hidden_in: bfloat16 [8192, 4608], P(('seq', 'tensor'))
- norm_gain: float32 [4608], replicated, may hold values from 0.5 to 1.5
- query_weight: bfloat16 [4608, 4096], P(None, 'tensor')
- key_weight: bfloat16 [4608, 2048], P(None, 'tensor'), may hold values from -0.09375 to 0.09375
- value_weight: bfloat16 [4608, 2048], P(None, 'tensor'), may hold values from -0.09375 to 0.09375
- out_weight: bfloat16 [4096, 4608], P('tensor'), may hold values from -0.09375 to 0.09375
- post_gain: float32 [4608], replicated, may hold values from 0.5 to 1.5
- seg_lengths: int32 [3], replicated, may hold values from 256 to 4096, as said below
- segment_ids: int32 [8192], replicated, may hold values from 0 to 2, as said below
- slot_map: int32 [3], replicated, may hold values from 0 to 2, each once
Outputs:
- hidden_out: bfloat16 [8192, 4608], P(('seq', 'tensor'))
- key_cache: bfloat16 [3, 4096, 2048], P(None, 'seq', 'tensor')
- value_cache: bfloat16 [3, 4096, 2048], P(None, 'seq', 'tensor')
The draws below stay inside these ranges and needn't reach their ends.
Inputs may be any that keep to these rules, and one draw needn't show every extreme that they name: `seg_lengths`: the 3 lengths sum to 8192; the second request is the longest, with exactly 4096 tokens. `segment_ids`: requests follow one another in order: request r holds seg_lengths[r] consecutive tokens, starting where request r - 1 ends. `slot_map`: each cache slot is named by exactly one request.
All inputs are finite; a program needn't handle non-finite values.
Results may differ from the reference program's by a relative error of at most 0.02.
Values may be sent and summed in bfloat16 or wider, within the bound.
No kernel may reach another device: no remote copies, remote signals or barrier semaphores. Data moves between devices by JAX's collectives and lax.ppermute only.
A program may use at most 128 MiB of HBM per device.

```python
import math
import jax
import jax.numpy as jnp
from jax import lax

D = 4608
HEADS = 32
KV_HEADS = 16
HD = 128
SEQS = 3
TOKENS = 8192
N_TENSOR = 32


def request_layout(key):
    base_key = jax.random.fold_in(key, 7)
    cut_key = jax.random.fold_in(base_key, 0)
    least = TOKENS // 32
    spare = TOKENS // 2 - 2 * least
    cut = jax.random.randint(cut_key, (), 0, spare + 1)
    others = least + jnp.stack([cut, spare - cut])
    ordinal = jnp.arange(SEQS, dtype=jnp.int32)
    picked = jnp.clip(ordinal - (ordinal > 1).astype(jnp.int32), 0, 1)
    lengths = jnp.where(ordinal == 1, TOKENS // 2, others[picked])
    return lengths.astype(jnp.int32)


def draw_seg_lengths(key, part):
    return request_layout(key)


def draw_segment_ids(key, part):
    lengths = request_layout(key)
    ends = jnp.cumsum(lengths)
    row_ids = jnp.arange(TOKENS, dtype=jnp.int32)
    return jnp.sum((row_ids[:, None] >= ends[None, :]).astype(jnp.int32), axis=1).astype(jnp.int32)


def draw_hidden_in(key, part):
    base_key, row_key, col_key = jax.random.split(key, 3)
    col_scale = jnp.exp(jax.random.uniform(col_key, (1, D), jnp.float32, math.log(0.3), math.log(3.0)))
    base = jnp.clip(jax.random.normal(base_key, (TOKENS, D), jnp.float32), -4.0, 4.0)
    row_scale = jnp.exp(jax.random.uniform(row_key, (TOKENS, 1), jnp.float32, math.log(0.3), math.log(3.0)))
    return (base * row_scale * col_scale).astype(jnp.bfloat16)


def draw_query_weight(key, part):
    base_key, head_key = jax.random.split(jax.random.fold_in(key, 11))
    head_scale = jnp.exp(jax.random.uniform(head_key, (HEADS,), jnp.float32, 0.0, math.log(8.0)))
    column_scale = jnp.repeat(head_scale, HD)
    base = jnp.clip(jax.random.normal(base_key, (D, HEADS * HD), jnp.float32), -4.0, 4.0)
    return (base * column_scale[None, :] * D ** (-0.5)).astype(jnp.bfloat16)


def steps_of(stream_key, shape, cuts, low, high):
    loudness = 1.0
    for axis_at, blocks in cuts:
        draws = jax.random.uniform(jax.random.fold_in(jax.random.fold_in(stream_key, 6), axis_at), (blocks,), jnp.float32, low / len(cuts), high / len(cuts))
        loudness = loudness * jnp.repeat(jnp.exp(draws), shape[axis_at] // blocks).reshape((-1,) + (1,) * (len(shape) - 1 - axis_at))
    return loudness


def scatter_about(key, dims, width, limit, pieces=(), kind=jnp.bfloat16):
    loudness = steps_of(key, dims, pieces, -0.22, 0.18) if pieces else 1.0
    values = jax.random.normal(key, dims, jnp.float32) * width * loudness
    return jnp.minimum(jnp.maximum(values, -limit), limit).astype(kind)


def setup_inputs(seed: int = 0) -> dict:
    key_of = jax.random.split(jax.random.key(seed), 11)
    hidden_in = draw_hidden_in(jax.random.fold_in(key_of[10], 71), 0)
    norm_gain = jnp.clip(1.0 + 0.1 * jax.random.normal(key_of[1], (D,), jnp.float32), 0.5, 1.5)
    query_weight = draw_query_weight(jax.random.fold_in(key_of[10], 71), 0)
    key_weight = scatter_about(key_of[3], (D, KV_HEADS * HD), D ** -0.5, 0.09375, ((1, 32),))
    value_weight = scatter_about(key_of[4], (D, KV_HEADS * HD), D ** -0.5, 0.09375, ((1, 32),))
    out_weight = scatter_about(key_of[5], (HEADS * HD, D), (HEADS * HD) ** -0.5, 0.09375, ((0, 32),))
    post_gain = jnp.clip(1.0 + 0.1 * jax.random.normal(key_of[6], (D,), jnp.float32), 0.5, 1.5)
    seg_lengths = draw_seg_lengths(jax.random.fold_in(key_of[10], 71), 0)
    segment_ids = draw_segment_ids(jax.random.fold_in(key_of[10], 71), 0)
    slot_map = jax.random.permutation(key_of[9], SEQS).astype(jnp.int32)
    return {"hidden_in": hidden_in, "norm_gain": norm_gain, "query_weight": query_weight, "key_weight": key_weight, "value_weight": value_weight, "out_weight": out_weight, "post_gain": post_gain, "seg_lengths": seg_lengths, "segment_ids": segment_ids, "slot_map": slot_map}


EPSILON = 1e-06
SOFTCAP = 50.0
QUERY_SCALE = 144.0 ** (-0.5)
SCORE_SHIFT = 20.0
ROPE_BASE = 10000.0

def rms_scale(values, gain):
    mean_sq = lax.optimization_barrier(jnp.mean(values * values, axis=-1, keepdims=True))
    return values * lax.rsqrt(mean_sq + EPSILON) * gain

def rotate(values, positions):
    head_dim = values.shape[-1]
    half_dim = head_dim // 2
    freqs = ROPE_BASE ** (-2.0 * jnp.arange(half_dim, dtype=jnp.float32) / head_dim)
    angles = positions.astype(jnp.float32)[:, None] * freqs[None, :]
    cosine = jnp.cos(angles)[:, None, :]
    sine = jnp.sin(angles)[:, None, :]
    first = values[..., :half_dim]
    second = values[..., half_dim:]
    return jnp.concatenate([first * cosine - second * sine, second * cosine + first * sine], axis=-1)

def token_positions(row_ids, row_segments, seg_lengths):
    starts = jnp.cumsum(seg_lengths) - seg_lengths
    request_ids = jnp.arange(seg_lengths.shape[0], dtype=jnp.int32)
    picked = lax.optimization_barrier(jnp.sum(jnp.where(row_segments[:, None] == request_ids[None, :], starts[None, :], 0), axis=1))
    return (row_ids - picked).astype(jnp.int32)

def reference(hidden_in, norm_gain, query_weight, key_weight, value_weight, out_weight, post_gain, seg_lengths, segment_ids, slot_map):
    tokens = hidden_in.shape[0]
    hidden = hidden_in.astype(jnp.float32)
    normed = rms_scale(hidden, norm_gain).astype(jnp.bfloat16)
    row_ids = jnp.arange(tokens, dtype=jnp.int32)
    positions = token_positions(row_ids, segment_ids, seg_lengths)
    queries = jnp.dot(normed, query_weight, preferred_element_type=jnp.float32).reshape(tokens, HEADS, HD)
    keys_raw = jnp.dot(normed, key_weight, preferred_element_type=jnp.float32).reshape(tokens, KV_HEADS, HD)
    values_bf = jnp.dot(normed, value_weight, preferred_element_type=jnp.float32).astype(jnp.bfloat16).reshape(tokens, KV_HEADS, HD)
    q_rot = rotate(queries, positions).astype(jnp.bfloat16)
    k_rot = rotate(keys_raw, positions).astype(jnp.bfloat16)
    block_rows = math.gcd(512, tokens)

    def one_head(head_index):
        q_head = lax.dynamic_index_in_dim(q_rot, head_index, 1, keepdims=False)
        k_head = lax.dynamic_index_in_dim(k_rot, head_index // 2, 1, keepdims=False)
        v_head = lax.dynamic_index_in_dim(values_bf, head_index // 2, 1, keepdims=False)

        def one_block(block_index):
            block_start = block_index * block_rows
            q_block = lax.dynamic_slice_in_dim(q_head, block_start, block_rows, 0)
            q_segments = lax.dynamic_slice_in_dim(segment_ids, block_start, block_rows, 0)
            q_rows = block_start + jnp.arange(block_rows, dtype=jnp.int32)
            scores = jnp.dot(q_block, k_head.T, preferred_element_type=jnp.float32) * QUERY_SCALE
            scores = SOFTCAP * jnp.tanh(scores / SOFTCAP)
            live = (row_ids[None, :] <= q_rows[:, None]) & (segment_ids[None, :] == q_segments[:, None])
            weights = jnp.where(live, jnp.exp(scores - SCORE_SHIFT), 0.0)
            totals = lax.optimization_barrier(jnp.sum(weights, axis=1, keepdims=True))
            mixed = jnp.dot(weights.astype(jnp.bfloat16), v_head, preferred_element_type=jnp.float32)
            return (mixed / totals).astype(jnp.bfloat16)
        blocks = lax.map(one_block, jnp.arange(tokens // block_rows, dtype=jnp.int32))
        return blocks.reshape(tokens, HD)
    heads_out = lax.map(one_head, jnp.arange(HEADS, dtype=jnp.int32))
    attended = jnp.transpose(heads_out, (1, 0, 2)).reshape(tokens, HEADS * HD)
    per_device = HEADS // N_TENSOR
    attn_groups = attended.reshape(tokens, N_TENSOR, per_device * HD)
    out_groups = out_weight.reshape(N_TENSOR, per_device * HD, D)

    def add_group(total, group_index):
        columns = lax.dynamic_index_in_dim(attn_groups, group_index, 1, keepdims=False)
        rows_w = lax.dynamic_index_in_dim(out_groups, group_index, 0, keepdims=False)
        partial_bf = jnp.dot(columns, rows_w, preferred_element_type=jnp.float32).astype(jnp.bfloat16)
        partial_bf = lax.optimization_barrier(partial_bf)
        return (total + partial_bf.astype(jnp.float32), None)
    projected, _ = lax.scan(add_group, jnp.zeros((tokens, D), jnp.float32), jnp.arange(N_TENSOR, dtype=jnp.int32))
    hidden_out = (hidden + rms_scale(projected, post_gain)).astype(jnp.bfloat16)
    cache_len = tokens // 2
    starts = (jnp.cumsum(seg_lengths) - seg_lengths).astype(jnp.int32)
    request_ids = jnp.arange(SEQS, dtype=jnp.int32)
    keys_flat = jnp.concatenate([k_rot.reshape(tokens, KV_HEADS * HD), jnp.zeros((cache_len, KV_HEADS * HD), jnp.bfloat16)], 0)
    values_flat = jnp.concatenate([values_bf.reshape(tokens, KV_HEADS * HD), jnp.zeros((cache_len, KV_HEADS * HD), jnp.bfloat16)], 0)
    seg_padded = jnp.concatenate([segment_ids, jnp.full((cache_len,), -1, jnp.int32)], 0)
    key_slots = []
    value_slots = []
    for slot_index in range(SEQS):
        request = jnp.sum(jnp.where(slot_map == slot_index, request_ids, 0)).astype(jnp.int32)
        first_row = jnp.sum(jnp.where(request_ids == request, starts, 0)).astype(jnp.int32)
        keep = lax.dynamic_slice_in_dim(seg_padded, first_row, cache_len, 0) == request
        key_slots.append(jnp.where(keep[:, None], lax.dynamic_slice_in_dim(keys_flat, first_row, cache_len, 0), jnp.zeros((), jnp.bfloat16)))
        value_slots.append(jnp.where(keep[:, None], lax.dynamic_slice_in_dim(values_flat, first_row, cache_len, 0), jnp.zeros((), jnp.bfloat16)))
    return (hidden_out, jnp.stack(key_slots), jnp.stack(value_slots))
```

```python
import jax
import jax.numpy as jnp
import numpy as np
from jax import lax
from jax.sharding import Mesh
from jax.sharding import PartitionSpec as P

HD = 128


EPSILON = 1e-06
SOFTCAP = 50.0
QUERY_SCALE = 144.0 ** (-0.5)
SCORE_SHIFT = 20.0
ROPE_BASE = 10000.0
KEY_TILE = 512
Q_CHUNKS = 2


def rms_scale(values, gain):
    mean_sq = jnp.mean(values * values, axis=-1, keepdims=True)
    return values * lax.rsqrt(mean_sq + EPSILON) * gain


def rotate(values, positions):
    head_dim = values.shape[-1]
    half_dim = head_dim // 2
    freqs = ROPE_BASE ** (-2.0 * jnp.arange(half_dim, dtype=jnp.float32) / head_dim)
    angles = positions.astype(jnp.float32)[:, None] * freqs[None, :]
    cosine = jnp.cos(angles)[:, None, :]
    sine = jnp.sin(angles)[:, None, :]
    first = values[..., :half_dim]
    second = values[..., half_dim:]
    return jnp.concatenate(
        [first * cosine - second * sine, second * cosine + first * sine], axis=-1
    )


def segment_starts_of(row_segments, seg_lengths):
    starts = jnp.cumsum(seg_lengths) - seg_lengths
    request_ids = jnp.arange(seg_lengths.shape[0], dtype=jnp.int32)
    return jnp.sum(
        jnp.where(row_segments[:, None] == request_ids[None, :], starts[None, :], 0), axis=1
    )


def swap(value, axis):
    return lax.ppermute(value, axis, [(0, 1), (1, 0)])


def on_device(
    hidden_in,
    norm_gain,
    query_weight,
    key_weight,
    value_weight,
    out_weight,
    post_gain,
    seg_lengths,
    segment_ids,
    slot_map,
):
    n_group = lax.axis_size("th")
    n_seq = lax.axis_size("seq")
    n_pair = lax.axis_size("tl")
    local_rows = hidden_in.shape[0]
    tokens = segment_ids.shape[0]
    group_rows = local_rows * n_group
    seq_rows = group_rows * n_pair
    head_dim = HD
    half_kv = key_weight.shape[1]
    seq_index = lax.axis_index("seq")
    pair_index = lax.axis_index("tl")
    slot_count = seg_lengths.shape[0]

    hidden = hidden_in.astype(jnp.float32)
    normed = rms_scale(hidden, norm_gain).astype(jnp.bfloat16)

    own_joined = jnp.concatenate([query_weight, key_weight, value_weight], axis=1)
    other_joined = swap(own_joined, "tl")
    other_out = swap(out_weight, "tl")

    spread = jnp.broadcast_to(normed[None], (n_group,) + normed.shape)
    gathered = lax.all_to_all(spread, "th", 0, 0, tiled=True).reshape(group_rows, -1)
    mixed = jnp.dot(
        gathered,
        jnp.concatenate([own_joined, other_joined], axis=1),
        preferred_element_type=jnp.float32,
    )
    width = own_joined.shape[1]
    q_own = mixed[:, :head_dim]
    k_own = mixed[:, head_dim : head_dim + half_kv]
    v_own = mixed[:, head_dim + half_kv : width]
    q_other = mixed[:, width : width + head_dim]
    k_other = mixed[:, width + head_dim : width + head_dim + half_kv]
    v_other = mixed[:, width + head_dim + half_kv :]
    leading = pair_index == 0
    full_key = jnp.where(
        leading, jnp.concatenate([k_own, k_other], 1), jnp.concatenate([k_other, k_own], 1)
    )
    full_value = jnp.where(
        leading, jnp.concatenate([v_own, v_other], 1), jnp.concatenate([v_other, v_own], 1)
    )

    member = jnp.arange(group_rows, dtype=jnp.int32) // local_rows
    within = jnp.arange(group_rows, dtype=jnp.int32) % local_rows
    row_ids = seq_index * seq_rows + (member * n_pair + pair_index) * local_rows + within
    row_segments = jnp.take(segment_ids, row_ids)
    positions = row_ids - segment_starts_of(row_segments, seg_lengths)

    q_rot = rotate(jnp.stack([q_own, q_other], axis=1), positions).astype(jnp.bfloat16)
    k_rot = rotate(full_key[:, None, :], positions)[:, 0].astype(jnp.bfloat16)
    v_bf = full_value.astype(jnp.bfloat16)

    kv = jnp.concatenate([k_rot, v_bf], axis=1)
    kv_all = lax.all_gather(kv, ("seq", "tl"), axis=0, tiled=True)
    kv_all = kv_all.reshape(n_seq, n_pair, n_group, local_rows, 2 * head_dim)
    kv_all = jnp.transpose(kv_all, (0, 2, 1, 3, 4)).reshape(tokens, 2 * head_dim)
    key_rows = kv_all[:, :head_dim]
    value_rows = kv_all[:, head_dim:]

    chunk_rows = group_rows // Q_CHUNKS
    q_chunks = q_rot.reshape(Q_CHUNKS, chunk_rows, 2, head_dim)
    q_ids = row_ids.reshape(Q_CHUNKS, chunk_rows)
    q_segs = row_segments.reshape(Q_CHUNKS, chunk_rows)
    zero_numer = jnp.zeros((chunk_rows, 2, head_dim), jnp.float32)
    zero_denom = jnp.zeros((2, chunk_rows), jnp.float32)
    start_state = (
        tuple(zero_numer for _ in range(Q_CHUNKS)),
        tuple(zero_denom for _ in range(Q_CHUNKS)),
    )
    first_needed = jnp.min(row_ids - positions)
    lo_tile = first_needed // KEY_TILE
    hi_tile = (jnp.max(row_ids) // KEY_TILE) + 1

    def tile(tile_index, state):
        numer, denom = state
        k_start = tile_index * KEY_TILE
        k_block = lax.dynamic_slice_in_dim(key_rows, k_start, KEY_TILE, 0)
        v_block = lax.dynamic_slice_in_dim(value_rows, k_start, KEY_TILE, 0)
        k_segs = lax.dynamic_slice_in_dim(segment_ids, k_start, KEY_TILE, 0)
        k_ids = k_start + jnp.arange(KEY_TILE, dtype=jnp.int32)
        new_numer = []
        new_denom = []
        for chunk in range(Q_CHUNKS):

            def compute(pair, chunk=chunk):
                numer_one, denom_one = pair
                scores = (
                    jnp.einsum(
                        "qhd,kd->hqk",
                        q_chunks[chunk],
                        k_block,
                        preferred_element_type=jnp.float32,
                    )
                    * QUERY_SCALE
                )
                scores = SOFTCAP * jnp.tanh(scores / SOFTCAP)
                live = (k_ids[None, :] <= q_ids[chunk][:, None]) & (
                    k_segs[None, :] == q_segs[chunk][:, None]
                )
                weights = jnp.where(live[None], jnp.exp(scores - SCORE_SHIFT), 0.0)
                denom_one = denom_one + jnp.sum(weights, axis=-1)
                numer_one = numer_one + jnp.einsum(
                    "hqk,kd->qhd",
                    weights.astype(jnp.bfloat16),
                    v_block,
                    preferred_element_type=jnp.float32,
                )
                return (numer_one, denom_one)

            useful = (
                (k_start <= q_ids[chunk][-1])
                & (k_segs[0] <= q_segs[chunk][-1])
                & (k_segs[-1] >= q_segs[chunk][0])
            )
            numer_one, denom_one = lax.cond(
                useful, compute, lambda pair: pair, (numer[chunk], denom[chunk])
            )
            new_numer.append(numer_one)
            new_denom.append(denom_one)
        return (tuple(new_numer), tuple(new_denom))

    numer, denom = lax.fori_loop(lo_tile, hi_tile, tile, start_state)
    finished = []
    for chunk in range(Q_CHUNKS):
        denom_rows = jnp.transpose(denom[chunk], (1, 0))[..., None]
        finished.append((numer[chunk] / denom_rows).astype(jnp.bfloat16))
    attended = jnp.concatenate(finished, axis=0).reshape(group_rows, 2 * head_dim)
    partial = jnp.dot(
        attended,
        jnp.concatenate([out_weight, other_out], axis=0),
        preferred_element_type=jnp.float32,
    ).astype(jnp.bfloat16)
    pieces = lax.all_to_all(
        partial.reshape(n_group, local_rows, -1), "th", 0, 0, tiled=True
    )
    projected = jnp.sum(pieces.astype(jnp.float32), axis=0)
    hidden_out = (hidden + rms_scale(projected, post_gain)).astype(jnp.bfloat16)

    cache_len = tokens // 2
    part_len = cache_len // n_seq
    request_ids = jnp.arange(slot_count, dtype=jnp.int32)
    starts = jnp.cumsum(seg_lengths) - seg_lengths
    own_offset = pair_index * half_kv
    own_keys = lax.dynamic_slice_in_dim(key_rows, own_offset, half_kv, 1)
    own_values = lax.dynamic_slice_in_dim(value_rows, own_offset, half_kv, 1)
    keys_pad = jnp.concatenate([own_keys, jnp.zeros((cache_len, half_kv), jnp.bfloat16)], 0)
    values_pad = jnp.concatenate(
        [own_values, jnp.zeros((cache_len, half_kv), jnp.bfloat16)], 0
    )
    seg_pad = jnp.concatenate([segment_ids, jnp.full((cache_len,), -1, jnp.int32)], 0)
    key_slots = []
    value_slots = []
    for slot_index in range(slot_count):
        request = jnp.sum(jnp.where(slot_map == slot_index, request_ids, 0)).astype(jnp.int32)
        first_row = jnp.sum(jnp.where(request_ids == request, starts, 0)).astype(jnp.int32)
        row0 = first_row + seq_index * part_len
        keep = (lax.dynamic_slice_in_dim(seg_pad, row0, part_len, 0) == request)[:, None]
        key_slots.append(
            jnp.where(
                keep,
                lax.dynamic_slice_in_dim(keys_pad, row0, part_len, 0),
                jnp.zeros((), jnp.bfloat16),
            )
        )
        value_slots.append(
            jnp.where(
                keep,
                lax.dynamic_slice_in_dim(values_pad, row0, part_len, 0),
                jnp.zeros((), jnp.bfloat16),
            )
        )
    return (hidden_out, jnp.stack(key_slots), jnp.stack(value_slots))


def solution(mesh):
    devices = np.asarray(mesh.devices)
    n_seq, n_tensor = devices.shape
    split = Mesh(devices.reshape(n_seq, n_tensor // 2, 2), ("seq", "th", "tl"))
    rows = P(("seq", "th", "tl"), None)
    cols = P(None, ("th", "tl"))
    return jax.shard_map(
        on_device,
        mesh=split,
        in_specs=(
            rows,
            P(),
            cols,
            cols,
            cols,
            P(("th", "tl"), None),
            P(),
            P(),
            P(),
            P(),
        ),
        out_specs=(rows, P(None, "seq", ("th", "tl")), P(None, "seq", ("th", "tl"))),
        check_vma=False,
    )
```

```python
import jax
import jax.numpy as jnp
import numpy as np
from jax import lax
from jax.sharding import Mesh
from jax.sharding import PartitionSpec as P

HD = 128


EPSILON = 1e-06
SOFTCAP = 50.0
QUERY_SCALE = 144.0 ** (-0.5)
SCORE_SHIFT = 20.0
ROPE_BASE = 10000.0
KEY_TILE = 512
Q_CHUNKS = 2


def rms_scale(values, gain):
    mean_sq = jnp.mean(values * values, axis=-1, keepdims=True)
    return values * lax.rsqrt(mean_sq + EPSILON) * gain


def rotate(values, positions):
    head_dim = values.shape[-1]
    half_dim = head_dim // 2
    freqs = ROPE_BASE ** (-2.0 * jnp.arange(half_dim, dtype=jnp.float32) / head_dim)
    angles = positions.astype(jnp.float32)[:, None] * freqs[None, :]
    cosine = jnp.cos(angles)[:, None, :]
    sine = jnp.sin(angles)[:, None, :]
    first = values[..., :half_dim]
    second = values[..., half_dim:]
    return jnp.concatenate(
        [first * cosine - second * sine, second * cosine + first * sine], axis=-1
    )


def segment_starts_of(row_segments, seg_lengths):
    starts = jnp.cumsum(seg_lengths) - seg_lengths
    request_ids = jnp.arange(seg_lengths.shape[0], dtype=jnp.int32)
    return jnp.sum(
        jnp.where(row_segments[:, None] == request_ids[None, :], starts[None, :], 0), axis=1
    )


def on_device(
    hidden_in,
    norm_gain,
    query_weight,
    key_weight,
    value_weight,
    out_weight,
    post_gain,
    seg_lengths,
    segment_ids,
    slot_map,
):
    n_group = lax.axis_size("th")
    n_seq = lax.axis_size("seq")
    n_pair = lax.axis_size("tl")
    local_rows = hidden_in.shape[0]
    tokens = segment_ids.shape[0]
    group_rows = local_rows * n_group
    seq_rows = group_rows * n_pair
    head_dim = HD
    half_kv = key_weight.shape[1]
    seq_index = lax.axis_index("seq")
    pair_index = lax.axis_index("tl")
    slot_count = seg_lengths.shape[0]

    hidden = hidden_in.astype(jnp.float32)
    normed = rms_scale(hidden, norm_gain).astype(jnp.bfloat16)

    own_joined = jnp.concatenate([query_weight, key_weight, value_weight], axis=1)
    pair_joined = lax.all_gather(own_joined, "tl", axis=0, tiled=False)
    pair_out = lax.all_gather(out_weight, "tl", axis=0, tiled=True)

    spread = jnp.broadcast_to(normed[None], (n_group,) + normed.shape)
    gathered = lax.all_to_all(spread, "th", 0, 0, tiled=True).reshape(group_rows, -1)
    mixed = jnp.dot(
        gathered,
        jnp.concatenate([pair_joined[0], pair_joined[1]], axis=1),
        preferred_element_type=jnp.float32,
    )
    width = own_joined.shape[1]
    q_first = mixed[:, :head_dim]
    q_second = mixed[:, width : width + head_dim]
    full_key = jnp.concatenate(
        [
            mixed[:, head_dim : head_dim + half_kv],
            mixed[:, width + head_dim : width + head_dim + half_kv],
        ],
        1,
    )
    full_value = jnp.concatenate(
        [mixed[:, head_dim + half_kv : width], mixed[:, width + head_dim + half_kv :]], 1
    )

    member = jnp.arange(group_rows, dtype=jnp.int32) // local_rows
    within = jnp.arange(group_rows, dtype=jnp.int32) % local_rows
    row_ids = seq_index * seq_rows + (member * n_pair + pair_index) * local_rows + within
    row_segments = jnp.take(segment_ids, row_ids)
    positions = row_ids - segment_starts_of(row_segments, seg_lengths)

    q_rot = rotate(jnp.stack([q_first, q_second], axis=1), positions).astype(jnp.bfloat16)
    k_rot = rotate(full_key[:, None, :], positions)[:, 0].astype(jnp.bfloat16)
    v_bf = full_value.astype(jnp.bfloat16)

    kv = jnp.concatenate([k_rot, v_bf], axis=1)
    kv_all = lax.all_gather(kv, ("seq", "tl"), axis=0, tiled=True)
    kv_all = kv_all.reshape(n_seq, n_pair, n_group, local_rows, 2 * head_dim)
    kv_all = jnp.transpose(kv_all, (0, 2, 1, 3, 4)).reshape(tokens, 2 * head_dim)
    key_rows = kv_all[:, :head_dim]
    value_rows = kv_all[:, head_dim:]

    chunk_rows = group_rows // Q_CHUNKS
    q_chunks = q_rot.reshape(Q_CHUNKS, chunk_rows, 2, head_dim)
    q_ids = row_ids.reshape(Q_CHUNKS, chunk_rows)
    q_segs = row_segments.reshape(Q_CHUNKS, chunk_rows)
    zero_numer = jnp.zeros((chunk_rows, 2, head_dim), jnp.float32)
    zero_denom = jnp.zeros((2, chunk_rows), jnp.float32)
    start_state = (
        tuple(zero_numer for _ in range(Q_CHUNKS)),
        tuple(zero_denom for _ in range(Q_CHUNKS)),
    )
    first_needed = jnp.min(row_ids - positions)
    lo_tile = first_needed // KEY_TILE
    hi_tile = (jnp.max(row_ids) // KEY_TILE) + 1

    def tile(tile_index, state):
        numer, denom = state
        k_start = tile_index * KEY_TILE
        k_block = lax.dynamic_slice_in_dim(key_rows, k_start, KEY_TILE, 0)
        v_block = lax.dynamic_slice_in_dim(value_rows, k_start, KEY_TILE, 0)
        k_segs = lax.dynamic_slice_in_dim(segment_ids, k_start, KEY_TILE, 0)
        k_ids = k_start + jnp.arange(KEY_TILE, dtype=jnp.int32)
        new_numer = []
        new_denom = []
        for chunk in range(Q_CHUNKS):

            def compute(pair, chunk=chunk):
                numer_one, denom_one = pair
                scores = (
                    jnp.einsum(
                        "qhd,kd->hqk",
                        q_chunks[chunk],
                        k_block,
                        preferred_element_type=jnp.float32,
                    )
                    * QUERY_SCALE
                )
                scores = SOFTCAP * jnp.tanh(scores / SOFTCAP)
                live = (k_ids[None, :] <= q_ids[chunk][:, None]) & (
                    k_segs[None, :] == q_segs[chunk][:, None]
                )
                weights = jnp.where(live[None], jnp.exp(scores - SCORE_SHIFT), 0.0)
                denom_one = denom_one + jnp.sum(weights, axis=-1)
                numer_one = numer_one + jnp.einsum(
                    "hqk,kd->qhd",
                    weights.astype(jnp.bfloat16),
                    v_block,
                    preferred_element_type=jnp.float32,
                )
                return (numer_one, denom_one)

            useful = (
                (k_start <= q_ids[chunk][-1])
                & (k_segs[0] <= q_segs[chunk][-1])
                & (k_segs[-1] >= q_segs[chunk][0])
            )
            numer_one, denom_one = lax.cond(
                useful, compute, lambda pair: pair, (numer[chunk], denom[chunk])
            )
            new_numer.append(numer_one)
            new_denom.append(denom_one)
        return (tuple(new_numer), tuple(new_denom))

    numer, denom = lax.fori_loop(lo_tile, hi_tile, tile, start_state)
    finished = []
    for chunk in range(Q_CHUNKS):
        denom_rows = jnp.transpose(denom[chunk], (1, 0))[..., None]
        finished.append((numer[chunk] / denom_rows).astype(jnp.bfloat16))
    attended = jnp.concatenate(finished, axis=0).reshape(group_rows, 2 * head_dim)
    partial = jnp.dot(
        attended,
        pair_out,
        preferred_element_type=jnp.float32,
    ).astype(jnp.bfloat16)
    pieces = lax.all_to_all(
        partial.reshape(n_group, local_rows, -1), "th", 0, 0, tiled=True
    )
    projected = jnp.sum(pieces.astype(jnp.float32), axis=0)
    hidden_out = (hidden + rms_scale(projected, post_gain)).astype(jnp.bfloat16)

    cache_len = tokens // 2
    part_len = cache_len // n_seq
    request_ids = jnp.arange(slot_count, dtype=jnp.int32)
    starts = jnp.cumsum(seg_lengths) - seg_lengths
    own_offset = pair_index * half_kv
    own_keys = lax.dynamic_slice_in_dim(key_rows, own_offset, half_kv, 1)
    own_values = lax.dynamic_slice_in_dim(value_rows, own_offset, half_kv, 1)
    keys_pad = jnp.concatenate([own_keys, jnp.zeros((cache_len, half_kv), jnp.bfloat16)], 0)
    values_pad = jnp.concatenate(
        [own_values, jnp.zeros((cache_len, half_kv), jnp.bfloat16)], 0
    )
    seg_pad = jnp.concatenate([segment_ids, jnp.full((cache_len,), -1, jnp.int32)], 0)
    key_slots = []
    value_slots = []
    for slot_index in range(slot_count):
        request = jnp.sum(jnp.where(slot_map == slot_index, request_ids, 0)).astype(jnp.int32)
        first_row = jnp.sum(jnp.where(request_ids == request, starts, 0)).astype(jnp.int32)
        row0 = first_row + seq_index * part_len
        keep = (lax.dynamic_slice_in_dim(seg_pad, row0, part_len, 0) == request)[:, None]
        key_slots.append(
            jnp.where(
                keep,
                lax.dynamic_slice_in_dim(keys_pad, row0, part_len, 0),
                jnp.zeros((), jnp.bfloat16),
            )
        )
        value_slots.append(
            jnp.where(
                keep,
                lax.dynamic_slice_in_dim(values_pad, row0, part_len, 0),
                jnp.zeros((), jnp.bfloat16),
            )
        )
    return (hidden_out, jnp.stack(key_slots), jnp.stack(value_slots))


def solution(mesh):
    devices = np.asarray(mesh.devices)
    n_seq, n_tensor = devices.shape
    split = Mesh(devices.reshape(n_seq, n_tensor // 2, 2), ("seq", "th", "tl"))
    rows = P(("seq", "th", "tl"), None)
    cols = P(None, ("th", "tl"))
    return jax.shard_map(
        on_device,
        mesh=split,
        in_specs=(
            rows,
            P(),
            cols,
            cols,
            cols,
            P(("th", "tl"), None),
            P(),
            P(),
            P(),
            P(),
        ),
        out_specs=(rows, P(None, "seq", ("th", "tl")), P(None, "seq", ("th", "tl"))),
        check_vma=False,
    )
```

```python
import jax
import jax.numpy as jnp
import numpy as np
from jax import lax
from jax.sharding import Mesh
from jax.sharding import PartitionSpec as P

HD = 128


EPSILON = 1e-06
SOFTCAP = 50.0
QUERY_SCALE = 144.0 ** (-0.5)
SCORE_SHIFT = 20.0
ROPE_BASE = 10000.0
KEY_TILE = 512
Q_CHUNKS = 2


def rms_scale(values, gain):
    mean_sq = jnp.mean(values * values, axis=-1, keepdims=True)
    return values * lax.rsqrt(mean_sq + EPSILON) * gain


def rotate(values, positions):
    head_dim = values.shape[-1]
    half_dim = head_dim // 2
    freqs = ROPE_BASE ** (-2.0 * jnp.arange(half_dim, dtype=jnp.float32) / head_dim)
    angles = positions.astype(jnp.float32)[:, None] * freqs[None, :]
    cosine = jnp.cos(angles)[:, None, :]
    sine = jnp.sin(angles)[:, None, :]
    first = values[..., :half_dim]
    second = values[..., half_dim:]
    return jnp.concatenate(
        [first * cosine - second * sine, second * cosine + first * sine], axis=-1
    )


def segment_starts_of(row_segments, seg_lengths):
    starts = jnp.cumsum(seg_lengths) - seg_lengths
    request_ids = jnp.arange(seg_lengths.shape[0], dtype=jnp.int32)
    return jnp.sum(
        jnp.where(row_segments[:, None] == request_ids[None, :], starts[None, :], 0), axis=1
    )


def on_device(
    hidden_in,
    norm_gain,
    query_weight,
    key_weight,
    value_weight,
    out_weight,
    post_gain,
    seg_lengths,
    segment_ids,
    slot_map,
):
    n_group = lax.axis_size("th")
    n_seq = lax.axis_size("seq")
    n_pair = lax.axis_size("tl")
    local_rows = hidden_in.shape[0]
    tokens = segment_ids.shape[0]
    group_rows = local_rows * n_group
    seq_rows = group_rows * n_pair
    head_dim = HD
    half_kv = key_weight.shape[1]
    seq_index = lax.axis_index("seq")
    pair_index = lax.axis_index("tl")
    slot_count = seg_lengths.shape[0]

    hidden = hidden_in.astype(jnp.float32)
    normed = rms_scale(hidden, norm_gain).astype(jnp.bfloat16)

    own_joined = jnp.concatenate([query_weight, key_weight, value_weight], axis=1)
    pair_joined = lax.all_gather(own_joined, "tl", axis=0, tiled=False)
    pair_out = lax.all_gather(out_weight, "tl", axis=0, tiled=True)

    spread = jnp.broadcast_to(normed[None], (n_group,) + normed.shape)
    gathered = lax.all_to_all(spread, "th", 0, 0, tiled=True).reshape(group_rows, -1)
    mixed = jnp.dot(
        gathered,
        jnp.concatenate([pair_joined[0], pair_joined[1]], axis=1),
        preferred_element_type=jnp.float32,
    )
    width = own_joined.shape[1]
    q_first = mixed[:, :head_dim]
    q_second = mixed[:, width : width + head_dim]
    full_key = jnp.concatenate(
        [
            mixed[:, head_dim : head_dim + half_kv],
            mixed[:, width + head_dim : width + head_dim + half_kv],
        ],
        1,
    )
    full_value = jnp.concatenate(
        [mixed[:, head_dim + half_kv : width], mixed[:, width + head_dim + half_kv :]], 1
    )

    member = jnp.arange(group_rows, dtype=jnp.int32) // local_rows
    within = jnp.arange(group_rows, dtype=jnp.int32) % local_rows
    row_ids = seq_index * seq_rows + (member * n_pair + pair_index) * local_rows + within
    row_segments = jnp.take(segment_ids, row_ids)
    positions = row_ids - segment_starts_of(row_segments, seg_lengths)

    q_rot = rotate(jnp.stack([q_first, q_second], axis=1), positions).astype(jnp.bfloat16)
    k_rot = rotate(full_key[:, None, :], positions)[:, 0].astype(jnp.bfloat16)
    v_bf = full_value.astype(jnp.bfloat16)

    kv = jnp.concatenate([k_rot, v_bf], axis=1)
    kv_all = lax.all_gather(kv, ("seq", "tl"), axis=0, tiled=True)
    kv_all = kv_all.reshape(n_seq, n_pair, n_group, local_rows, 2 * head_dim)
    kv_all = jnp.transpose(kv_all, (0, 2, 1, 3, 4)).reshape(tokens, 2 * head_dim)
    key_rows = kv_all[:, :head_dim]
    value_rows = kv_all[:, head_dim:]

    chunk_rows = group_rows // Q_CHUNKS
    member_part = local_rows // Q_CHUNKS
    q_chunks = jnp.transpose(
        q_rot.reshape(n_group, Q_CHUNKS, member_part, 2, head_dim), (1, 0, 2, 3, 4)
    ).reshape(Q_CHUNKS, chunk_rows, 2, head_dim)
    q_ids = jnp.transpose(row_ids.reshape(n_group, Q_CHUNKS, member_part), (1, 0, 2)).reshape(
        Q_CHUNKS, chunk_rows
    )
    q_segs = jnp.transpose(
        row_segments.reshape(n_group, Q_CHUNKS, member_part), (1, 0, 2)
    ).reshape(Q_CHUNKS, chunk_rows)
    first_needed = jnp.min(row_ids - positions)
    lo_tile = first_needed // KEY_TILE
    hi_tile = (jnp.max(row_ids) // KEY_TILE) + 1

    def attend(chunk):
        def tile(tile_index, state):
            numer_one, denom_one = state
            k_start = tile_index * KEY_TILE
            k_block = lax.dynamic_slice_in_dim(key_rows, k_start, KEY_TILE, 0)
            v_block = lax.dynamic_slice_in_dim(value_rows, k_start, KEY_TILE, 0)
            k_segs = lax.dynamic_slice_in_dim(segment_ids, k_start, KEY_TILE, 0)
            k_ids = k_start + jnp.arange(KEY_TILE, dtype=jnp.int32)

            def compute(pair):
                numer_one, denom_one = pair
                scores = (
                    jnp.einsum(
                        "qhd,kd->hqk",
                        q_chunks[chunk],
                        k_block,
                        preferred_element_type=jnp.float32,
                    )
                    * QUERY_SCALE
                )
                scores = SOFTCAP * jnp.tanh(scores / SOFTCAP)
                live = (k_ids[None, :] <= q_ids[chunk][:, None]) & (
                    k_segs[None, :] == q_segs[chunk][:, None]
                )
                weights = jnp.where(live[None], jnp.exp(scores - SCORE_SHIFT), 0.0)
                denom_one = denom_one + jnp.sum(weights, axis=-1)
                numer_one = numer_one + jnp.einsum(
                    "hqk,kd->qhd",
                    weights.astype(jnp.bfloat16),
                    v_block,
                    preferred_element_type=jnp.float32,
                )
                return (numer_one, denom_one)

            useful = (
                (k_start <= q_ids[chunk][-1])
                & (k_segs[0] <= q_segs[chunk][-1])
                & (k_segs[-1] >= q_segs[chunk][0])
            )
            return lax.cond(useful, compute, lambda pair: pair, (numer_one, denom_one))

        zero_numer = jnp.zeros((chunk_rows, 2, head_dim), jnp.float32)
        zero_denom = jnp.zeros((2, chunk_rows), jnp.float32)
        numer, denom = lax.fori_loop(lo_tile, hi_tile, tile, (zero_numer, zero_denom))
        denom_rows = jnp.transpose(denom, (1, 0))[..., None]
        attended = (numer / denom_rows).astype(jnp.bfloat16).reshape(chunk_rows, 2 * head_dim)
        partial = jnp.dot(attended, pair_out, preferred_element_type=jnp.float32).astype(
            jnp.bfloat16
        )
        pieces = lax.all_to_all(
            partial.reshape(n_group, member_part, -1), "th", 0, 0, tiled=True
        )
        return jnp.sum(pieces.astype(jnp.float32), axis=0)

    projected = jnp.concatenate([attend(chunk) for chunk in range(Q_CHUNKS)], axis=0)
    hidden_out = (hidden + rms_scale(projected, post_gain)).astype(jnp.bfloat16)

    cache_len = tokens // 2
    part_len = cache_len // n_seq
    request_ids = jnp.arange(slot_count, dtype=jnp.int32)
    starts = jnp.cumsum(seg_lengths) - seg_lengths
    own_offset = pair_index * half_kv
    own_keys = lax.dynamic_slice_in_dim(key_rows, own_offset, half_kv, 1)
    own_values = lax.dynamic_slice_in_dim(value_rows, own_offset, half_kv, 1)
    keys_pad = jnp.concatenate([own_keys, jnp.zeros((cache_len, half_kv), jnp.bfloat16)], 0)
    values_pad = jnp.concatenate(
        [own_values, jnp.zeros((cache_len, half_kv), jnp.bfloat16)], 0
    )
    seg_pad = jnp.concatenate([segment_ids, jnp.full((cache_len,), -1, jnp.int32)], 0)
    key_slots = []
    value_slots = []
    for slot_index in range(slot_count):
        request = jnp.sum(jnp.where(slot_map == slot_index, request_ids, 0)).astype(jnp.int32)
        first_row = jnp.sum(jnp.where(request_ids == request, starts, 0)).astype(jnp.int32)
        row0 = first_row + seq_index * part_len
        keep = (lax.dynamic_slice_in_dim(seg_pad, row0, part_len, 0) == request)[:, None]
        key_slots.append(
            jnp.where(
                keep,
                lax.dynamic_slice_in_dim(keys_pad, row0, part_len, 0),
                jnp.zeros((), jnp.bfloat16),
            )
        )
        value_slots.append(
            jnp.where(
                keep,
                lax.dynamic_slice_in_dim(values_pad, row0, part_len, 0),
                jnp.zeros((), jnp.bfloat16),
            )
        )
    return (hidden_out, jnp.stack(key_slots), jnp.stack(value_slots))


def solution(mesh):
    devices = np.asarray(mesh.devices)
    n_seq, n_tensor = devices.shape
    split = Mesh(devices.reshape(n_seq, n_tensor // 2, 2), ("seq", "th", "tl"))
    rows = P(("seq", "th", "tl"), None)
    cols = P(None, ("th", "tl"))
    return jax.shard_map(
        on_device,
        mesh=split,
        in_specs=(
            rows,
            P(),
            cols,
            cols,
            cols,
            P(("th", "tl"), None),
            P(),
            P(),
            P(),
            P(),
        ),
        out_specs=(rows, P(None, "seq", ("th", "tl")), P(None, "seq", ("th", "tl"))),
        check_vma=False,
    )
```

```python
import jax
import jax.numpy as jnp
import numpy as np
from jax import lax
from jax.sharding import Mesh
from jax.sharding import PartitionSpec as P

HD = 128


EPSILON = 1e-06
SOFTCAP = 50.0
QUERY_SCALE = 144.0 ** (-0.5)
SCORE_SHIFT = 20.0
ROPE_BASE = 10000.0
KEY_TILE = 512
Q_CHUNKS = 2


def rms_scale(values, gain):
    mean_sq = jnp.mean(values * values, axis=-1, keepdims=True)
    return values * lax.rsqrt(mean_sq + EPSILON) * gain


def rotate(values, positions):
    head_dim = values.shape[-1]
    half_dim = head_dim // 2
    freqs = ROPE_BASE ** (-2.0 * jnp.arange(half_dim, dtype=jnp.float32) / head_dim)
    angles = positions.astype(jnp.float32)[:, None] * freqs[None, :]
    cosine = jnp.cos(angles)[:, None, :]
    sine = jnp.sin(angles)[:, None, :]
    first = values[..., :half_dim]
    second = values[..., half_dim:]
    return jnp.concatenate(
        [first * cosine - second * sine, second * cosine + first * sine], axis=-1
    )


def segment_starts_of(row_segments, seg_lengths):
    starts = jnp.cumsum(seg_lengths) - seg_lengths
    request_ids = jnp.arange(seg_lengths.shape[0], dtype=jnp.int32)
    return jnp.sum(
        jnp.where(row_segments[:, None] == request_ids[None, :], starts[None, :], 0), axis=1
    )


def on_device(
    hidden_in,
    norm_gain,
    query_weight,
    key_weight,
    value_weight,
    out_weight,
    post_gain,
    seg_lengths,
    segment_ids,
    slot_map,
):
    n_group = lax.axis_size("th")
    n_seq = lax.axis_size("seq")
    n_pair = lax.axis_size("tl")
    local_rows = hidden_in.shape[0]
    tokens = segment_ids.shape[0]
    group_rows = local_rows * n_group
    seq_rows = group_rows * n_pair
    head_dim = HD
    half_kv = key_weight.shape[1]
    seq_index = lax.axis_index("seq")
    pair_index = lax.axis_index("tl")
    slot_count = seg_lengths.shape[0]

    hidden = hidden_in.astype(jnp.float32)
    normed = rms_scale(hidden, norm_gain).astype(jnp.bfloat16)

    own_joined = jnp.concatenate([query_weight, key_weight, value_weight], axis=1)
    pair_joined = lax.all_gather(own_joined, "tl", axis=0, tiled=False)
    pair_out = lax.all_gather(out_weight, "tl", axis=0, tiled=True)

    spread = jnp.broadcast_to(normed[None], (n_group,) + normed.shape)
    gathered = lax.all_to_all(spread, "th", 0, 0, tiled=True).reshape(group_rows, -1)
    mixed = jnp.dot(
        gathered,
        jnp.concatenate([pair_joined[0], pair_joined[1]], axis=1),
        preferred_element_type=jnp.float32,
    )
    width = own_joined.shape[1]
    q_first = mixed[:, :head_dim]
    q_second = mixed[:, width : width + head_dim]
    full_key = jnp.concatenate(
        [
            mixed[:, head_dim : head_dim + half_kv],
            mixed[:, width + head_dim : width + head_dim + half_kv],
        ],
        1,
    )
    full_value = jnp.concatenate(
        [mixed[:, head_dim + half_kv : width], mixed[:, width + head_dim + half_kv :]], 1
    )

    member = jnp.arange(group_rows, dtype=jnp.int32) // local_rows
    within = jnp.arange(group_rows, dtype=jnp.int32) % local_rows
    row_ids = seq_index * seq_rows + (member * n_pair + pair_index) * local_rows + within
    row_segments = jnp.take(segment_ids, row_ids)
    positions = row_ids - segment_starts_of(row_segments, seg_lengths)

    q_rot = rotate(jnp.stack([q_first, q_second], axis=1), positions).astype(jnp.bfloat16)
    k_rot = rotate(full_key[:, None, :], positions)[:, 0].astype(jnp.bfloat16)
    v_bf = full_value.astype(jnp.bfloat16)

    kv = jnp.concatenate([k_rot, v_bf], axis=1)
    kv_all = lax.all_gather(kv, ("seq", "tl"), axis=0, tiled=True)
    kv_all = kv_all.reshape(n_seq, n_pair, n_group, local_rows, 2 * head_dim)
    kv_all = jnp.transpose(kv_all, (0, 2, 1, 3, 4)).reshape(tokens, 2 * head_dim)
    key_rows = kv_all[:, :head_dim]
    value_rows = kv_all[:, head_dim:]

    chunk_rows = group_rows // Q_CHUNKS
    member_part = local_rows // Q_CHUNKS
    q_chunks = jnp.transpose(
        q_rot.reshape(n_group, Q_CHUNKS, member_part, 2, head_dim), (1, 0, 2, 3, 4)
    ).reshape(Q_CHUNKS, chunk_rows, 2, head_dim)
    q_ids = jnp.transpose(row_ids.reshape(n_group, Q_CHUNKS, member_part), (1, 0, 2)).reshape(
        Q_CHUNKS, chunk_rows
    )
    q_segs = jnp.transpose(
        row_segments.reshape(n_group, Q_CHUNKS, member_part), (1, 0, 2)
    ).reshape(Q_CHUNKS, chunk_rows)
    q_pos = jnp.transpose(positions.reshape(n_group, Q_CHUNKS, member_part), (1, 0, 2)).reshape(
        Q_CHUNKS, chunk_rows
    )

    def attend(chunk):
        def tile(tile_index, state):
            numer_one, denom_one = state
            k_start = tile_index * KEY_TILE
            k_block = lax.dynamic_slice_in_dim(key_rows, k_start, KEY_TILE, 0)
            v_block = lax.dynamic_slice_in_dim(value_rows, k_start, KEY_TILE, 0)
            k_segs = lax.dynamic_slice_in_dim(segment_ids, k_start, KEY_TILE, 0)
            k_ids = k_start + jnp.arange(KEY_TILE, dtype=jnp.int32)

            scores = (
                jnp.einsum(
                    "qhd,kd->hqk",
                    q_chunks[chunk],
                    k_block,
                    preferred_element_type=jnp.float32,
                )
                * QUERY_SCALE
            )
            scores = SOFTCAP * jnp.tanh(scores / SOFTCAP)
            live = (k_ids[None, :] <= q_ids[chunk][:, None]) & (
                k_segs[None, :] == q_segs[chunk][:, None]
            )
            weights = jnp.where(live[None], jnp.exp(scores - SCORE_SHIFT), 0.0)
            denom_one = denom_one + jnp.sum(weights, axis=-1)
            numer_one = numer_one + jnp.einsum(
                "hqk,kd->qhd",
                weights.astype(jnp.bfloat16),
                v_block,
                preferred_element_type=jnp.float32,
            )
            return (numer_one, denom_one)

        zero_numer = jnp.zeros((chunk_rows, 2, head_dim), jnp.float32)
        zero_denom = jnp.zeros((2, chunk_rows), jnp.float32)
        lo_tile = jnp.min(q_ids[chunk] - q_pos[chunk]) // KEY_TILE
        hi_tile = jnp.max(q_ids[chunk]) // KEY_TILE + 1
        numer, denom = lax.fori_loop(lo_tile, hi_tile, tile, (zero_numer, zero_denom))
        denom_rows = jnp.transpose(denom, (1, 0))[..., None]
        attended = (numer / denom_rows).astype(jnp.bfloat16).reshape(chunk_rows, 2 * head_dim)
        partial = jnp.dot(attended, pair_out, preferred_element_type=jnp.float32).astype(
            jnp.bfloat16
        )
        pieces = lax.all_to_all(
            partial.reshape(n_group, member_part, -1), "th", 0, 0, tiled=True
        )
        return jnp.sum(pieces.astype(jnp.float32), axis=0)

    projected = jnp.concatenate([attend(chunk) for chunk in range(Q_CHUNKS)], axis=0)
    hidden_out = (hidden + rms_scale(projected, post_gain)).astype(jnp.bfloat16)

    cache_len = tokens // 2
    part_len = cache_len // n_seq
    request_ids = jnp.arange(slot_count, dtype=jnp.int32)
    starts = jnp.cumsum(seg_lengths) - seg_lengths
    own_offset = pair_index * half_kv
    own_keys = lax.dynamic_slice_in_dim(key_rows, own_offset, half_kv, 1)
    own_values = lax.dynamic_slice_in_dim(value_rows, own_offset, half_kv, 1)
    keys_pad = jnp.concatenate([own_keys, jnp.zeros((cache_len, half_kv), jnp.bfloat16)], 0)
    values_pad = jnp.concatenate(
        [own_values, jnp.zeros((cache_len, half_kv), jnp.bfloat16)], 0
    )
    seg_pad = jnp.concatenate([segment_ids, jnp.full((cache_len,), -1, jnp.int32)], 0)
    key_slots = []
    value_slots = []
    for slot_index in range(slot_count):
        request = jnp.sum(jnp.where(slot_map == slot_index, request_ids, 0)).astype(jnp.int32)
        first_row = jnp.sum(jnp.where(request_ids == request, starts, 0)).astype(jnp.int32)
        row0 = first_row + seq_index * part_len
        keep = (lax.dynamic_slice_in_dim(seg_pad, row0, part_len, 0) == request)[:, None]
        key_slots.append(
            jnp.where(
                keep,
                lax.dynamic_slice_in_dim(keys_pad, row0, part_len, 0),
                jnp.zeros((), jnp.bfloat16),
            )
        )
        value_slots.append(
            jnp.where(
                keep,
                lax.dynamic_slice_in_dim(values_pad, row0, part_len, 0),
                jnp.zeros((), jnp.bfloat16),
            )
        )
    return (hidden_out, jnp.stack(key_slots), jnp.stack(value_slots))


def solution(mesh):
    devices = np.asarray(mesh.devices)
    n_seq, n_tensor = devices.shape
    split = Mesh(devices.reshape(n_seq, n_tensor // 2, 2), ("seq", "th", "tl"))
    rows = P(("seq", "th", "tl"), None)
    cols = P(None, ("th", "tl"))
    return jax.shard_map(
        on_device,
        mesh=split,
        in_specs=(
            rows,
            P(),
            cols,
            cols,
            cols,
            P(("th", "tl"), None),
            P(),
            P(),
            P(),
            P(),
        ),
        out_specs=(rows, P(None, "seq", ("th", "tl")), P(None, "seq", ("th", "tl"))),
        check_vma=False,
    )
```

```python
import jax
import jax.numpy as jnp
import numpy as np
from jax import lax
from jax.sharding import Mesh
from jax.sharding import PartitionSpec as P

HD = 128


EPSILON = 1e-06
SOFTCAP = 50.0
QUERY_SCALE = 144.0 ** (-0.5)
SCORE_SHIFT = 20.0
ROPE_BASE = 10000.0
KEY_TILE = 512
Q_CHUNKS = 2


def rms_scale(values, gain):
    mean_sq = jnp.mean(values * values, axis=-1, keepdims=True)
    return values * lax.rsqrt(mean_sq + EPSILON) * gain


def rotate(values, positions):
    head_dim = values.shape[-1]
    half_dim = head_dim // 2
    freqs = ROPE_BASE ** (-2.0 * jnp.arange(half_dim, dtype=jnp.float32) / head_dim)
    angles = positions.astype(jnp.float32)[:, None] * freqs[None, :]
    cosine = jnp.cos(angles)[:, None, :]
    sine = jnp.sin(angles)[:, None, :]
    first = values[..., :half_dim]
    second = values[..., half_dim:]
    return jnp.concatenate(
        [first * cosine - second * sine, second * cosine + first * sine], axis=-1
    )


def segment_starts_of(row_segments, seg_lengths):
    starts = jnp.cumsum(seg_lengths) - seg_lengths
    request_ids = jnp.arange(seg_lengths.shape[0], dtype=jnp.int32)
    return jnp.sum(
        jnp.where(row_segments[:, None] == request_ids[None, :], starts[None, :], 0), axis=1
    )


def on_device(
    hidden_in,
    norm_gain,
    query_weight,
    key_weight,
    value_weight,
    out_weight,
    post_gain,
    seg_lengths,
    segment_ids,
    slot_map,
):
    n_group = lax.axis_size("th")
    n_seq = lax.axis_size("seq")
    n_pair = lax.axis_size("tl")
    local_rows = hidden_in.shape[0]
    tokens = segment_ids.shape[0]
    group_rows = local_rows * n_group
    seq_rows = group_rows * n_pair
    head_dim = HD
    half_kv = key_weight.shape[1]
    seq_index = lax.axis_index("seq")
    pair_index = lax.axis_index("tl")
    slot_count = seg_lengths.shape[0]

    hidden = hidden_in.astype(jnp.float32)
    normed = rms_scale(hidden, norm_gain).astype(jnp.bfloat16)

    own_joined = jnp.concatenate([query_weight, key_weight, value_weight], axis=1)
    pair_joined = lax.all_gather(own_joined, "tl", axis=0, tiled=False)
    pair_out = lax.all_gather(out_weight, "tl", axis=0, tiled=True)

    spread = jnp.broadcast_to(normed[None], (n_group,) + normed.shape)
    spread, pair_joined = lax.optimization_barrier((spread, pair_joined))
    gathered = lax.all_to_all(spread, "th", 0, 0, tiled=True).reshape(group_rows, -1)
    mixed = jnp.dot(
        gathered,
        jnp.concatenate([pair_joined[0], pair_joined[1]], axis=1),
        preferred_element_type=jnp.float32,
    )
    width = own_joined.shape[1]
    q_first = mixed[:, :head_dim]
    q_second = mixed[:, width : width + head_dim]
    full_key = jnp.concatenate(
        [
            mixed[:, head_dim : head_dim + half_kv],
            mixed[:, width + head_dim : width + head_dim + half_kv],
        ],
        1,
    )
    full_value = jnp.concatenate(
        [mixed[:, head_dim + half_kv : width], mixed[:, width + head_dim + half_kv :]], 1
    )

    member = jnp.arange(group_rows, dtype=jnp.int32) // local_rows
    within = jnp.arange(group_rows, dtype=jnp.int32) % local_rows
    row_ids = seq_index * seq_rows + (member * n_pair + pair_index) * local_rows + within
    row_segments = jnp.take(segment_ids, row_ids)
    positions = row_ids - segment_starts_of(row_segments, seg_lengths)

    q_rot = rotate(jnp.stack([q_first, q_second], axis=1), positions).astype(jnp.bfloat16)
    k_rot = rotate(full_key[:, None, :], positions)[:, 0].astype(jnp.bfloat16)
    v_bf = full_value.astype(jnp.bfloat16)

    kv = jnp.concatenate([k_rot, v_bf], axis=1)
    kv_all = lax.all_gather(kv, ("seq", "tl"), axis=0, tiled=True)
    kv_all = kv_all.reshape(n_seq, n_pair, n_group, local_rows, 2 * head_dim)
    kv_all = jnp.transpose(kv_all, (0, 2, 1, 3, 4)).reshape(tokens, 2 * head_dim)
    key_rows = kv_all[:, :head_dim]
    value_rows = kv_all[:, head_dim:]

    chunk_rows = group_rows // Q_CHUNKS
    member_part = local_rows // Q_CHUNKS
    q_chunks = jnp.transpose(
        q_rot.reshape(n_group, Q_CHUNKS, member_part, 2, head_dim), (1, 0, 2, 3, 4)
    ).reshape(Q_CHUNKS, chunk_rows, 2, head_dim)
    q_ids = jnp.transpose(row_ids.reshape(n_group, Q_CHUNKS, member_part), (1, 0, 2)).reshape(
        Q_CHUNKS, chunk_rows
    )
    q_segs = jnp.transpose(
        row_segments.reshape(n_group, Q_CHUNKS, member_part), (1, 0, 2)
    ).reshape(Q_CHUNKS, chunk_rows)
    q_pos = jnp.transpose(positions.reshape(n_group, Q_CHUNKS, member_part), (1, 0, 2)).reshape(
        Q_CHUNKS, chunk_rows
    )

    def attend(chunk):
        def tile(tile_index, state):
            numer_one, denom_one = state
            k_start = tile_index * KEY_TILE
            k_block = lax.dynamic_slice_in_dim(key_rows, k_start, KEY_TILE, 0)
            v_block = lax.dynamic_slice_in_dim(value_rows, k_start, KEY_TILE, 0)
            k_segs = lax.dynamic_slice_in_dim(segment_ids, k_start, KEY_TILE, 0)
            k_ids = k_start + jnp.arange(KEY_TILE, dtype=jnp.int32)

            scores = (
                jnp.einsum(
                    "qhd,kd->hqk",
                    q_chunks[chunk],
                    k_block,
                    preferred_element_type=jnp.float32,
                )
                * QUERY_SCALE
            )
            scores = SOFTCAP * jnp.tanh(scores / SOFTCAP)
            live = (k_ids[None, :] <= q_ids[chunk][:, None]) & (
                k_segs[None, :] == q_segs[chunk][:, None]
            )
            weights = jnp.where(live[None], jnp.exp(scores - SCORE_SHIFT), 0.0)
            denom_one = denom_one + jnp.sum(weights, axis=-1)
            numer_one = numer_one + jnp.einsum(
                "hqk,kd->qhd",
                weights.astype(jnp.bfloat16),
                v_block,
                preferred_element_type=jnp.float32,
            )
            return (numer_one, denom_one)

        zero_numer = jnp.zeros((chunk_rows, 2, head_dim), jnp.float32)
        zero_denom = jnp.zeros((2, chunk_rows), jnp.float32)
        lo_tile = jnp.min(q_ids[chunk] - q_pos[chunk]) // KEY_TILE
        hi_tile = jnp.max(q_ids[chunk]) // KEY_TILE + 1
        numer, denom = lax.fori_loop(lo_tile, hi_tile, tile, (zero_numer, zero_denom))
        denom_rows = jnp.transpose(denom, (1, 0))[..., None]
        attended = (numer / denom_rows).astype(jnp.bfloat16).reshape(chunk_rows, 2 * head_dim)
        partial = jnp.dot(attended, pair_out, preferred_element_type=jnp.float32).astype(
            jnp.bfloat16
        )
        pieces = lax.all_to_all(
            partial.reshape(n_group, member_part, -1), "th", 0, 0, tiled=True
        )
        return jnp.sum(pieces.astype(jnp.float32), axis=0)

    projected = jnp.concatenate([attend(chunk) for chunk in range(Q_CHUNKS)], axis=0)
    hidden_out = (hidden + rms_scale(projected, post_gain)).astype(jnp.bfloat16)

    cache_len = tokens // 2
    part_len = cache_len // n_seq
    request_ids = jnp.arange(slot_count, dtype=jnp.int32)
    starts = jnp.cumsum(seg_lengths) - seg_lengths
    own_offset = pair_index * half_kv
    own_keys = lax.dynamic_slice_in_dim(key_rows, own_offset, half_kv, 1)
    own_values = lax.dynamic_slice_in_dim(value_rows, own_offset, half_kv, 1)
    keys_pad = jnp.concatenate([own_keys, jnp.zeros((cache_len, half_kv), jnp.bfloat16)], 0)
    values_pad = jnp.concatenate(
        [own_values, jnp.zeros((cache_len, half_kv), jnp.bfloat16)], 0
    )
    seg_pad = jnp.concatenate([segment_ids, jnp.full((cache_len,), -1, jnp.int32)], 0)
    key_slots = []
    value_slots = []
    for slot_index in range(slot_count):
        request = jnp.sum(jnp.where(slot_map == slot_index, request_ids, 0)).astype(jnp.int32)
        first_row = jnp.sum(jnp.where(request_ids == request, starts, 0)).astype(jnp.int32)
        row0 = first_row + seq_index * part_len
        keep = (lax.dynamic_slice_in_dim(seg_pad, row0, part_len, 0) == request)[:, None]
        key_slots.append(
            jnp.where(
                keep,
                lax.dynamic_slice_in_dim(keys_pad, row0, part_len, 0),
                jnp.zeros((), jnp.bfloat16),
            )
        )
        value_slots.append(
            jnp.where(
                keep,
                lax.dynamic_slice_in_dim(values_pad, row0, part_len, 0),
                jnp.zeros((), jnp.bfloat16),
            )
        )
    return (hidden_out, jnp.stack(key_slots), jnp.stack(value_slots))


def solution(mesh):
    devices = np.asarray(mesh.devices)
    n_seq, n_tensor = devices.shape
    split = Mesh(devices.reshape(n_seq, n_tensor // 2, 2), ("seq", "th", "tl"))
    rows = P(("seq", "th", "tl"), None)
    cols = P(None, ("th", "tl"))
    return jax.shard_map(
        on_device,
        mesh=split,
        in_specs=(
            rows,
            P(),
            cols,
            cols,
            cols,
            P(("th", "tl"), None),
            P(),
            P(),
            P(),
            P(),
        ),
        out_specs=(rows, P(None, "seq", ("th", "tl")), P(None, "seq", ("th", "tl"))),
        check_vma=False,
    )
```

```python
import jax
import jax.numpy as jnp
import numpy as np
from jax import lax
from jax.sharding import Mesh
from jax.sharding import PartitionSpec as P

HD = 128


EPSILON = 1e-06
SOFTCAP = 50.0
QUERY_SCALE = 144.0 ** (-0.5)
SCORE_SHIFT = 20.0
ROPE_BASE = 10000.0
KEY_TILE = 512
Q_CHUNKS = 2
HEADS_PER_DEVICE = 4


def rms_scale(values, gain):
    mean_sq = jnp.mean(values * values, axis=-1, keepdims=True)
    return values * lax.rsqrt(mean_sq + EPSILON) * gain


def rotate(values, positions):
    head_dim = values.shape[-1]
    half_dim = head_dim // 2
    freqs = ROPE_BASE ** (-2.0 * jnp.arange(half_dim, dtype=jnp.float32) / head_dim)
    angles = positions.astype(jnp.float32)[:, None] * freqs[None, :]
    cosine = jnp.cos(angles)[:, None, :]
    sine = jnp.sin(angles)[:, None, :]
    first = values[..., :half_dim]
    second = values[..., half_dim:]
    return jnp.concatenate(
        [first * cosine - second * sine, second * cosine + first * sine], axis=-1
    )


def segment_starts_of(row_segments, seg_lengths):
    starts = jnp.cumsum(seg_lengths) - seg_lengths
    request_ids = jnp.arange(seg_lengths.shape[0], dtype=jnp.int32)
    return jnp.sum(
        jnp.where(row_segments[:, None] == request_ids[None, :], starts[None, :], 0), axis=1
    )


def on_device(
    hidden_in,
    norm_gain,
    query_weight,
    key_weight,
    value_weight,
    out_weight,
    post_gain,
    seg_lengths,
    segment_ids,
    slot_map,
):
    n_group = lax.axis_size("th")
    n_seq = lax.axis_size("seq")
    n_pair = lax.axis_size("tl")
    kv_local = n_pair // 2
    local_rows = hidden_in.shape[0]
    tokens = segment_ids.shape[0]
    group_rows = local_rows * n_group
    seq_rows = group_rows * n_pair
    head_dim = HD
    half_kv = key_weight.shape[1]
    seq_index = lax.axis_index("seq")
    pair_index = lax.axis_index("tl")
    slot_count = seg_lengths.shape[0]

    hidden = hidden_in.astype(jnp.float32)
    normed = rms_scale(hidden, norm_gain).astype(jnp.bfloat16)

    own_joined = jnp.concatenate([query_weight, key_weight, value_weight], axis=1)
    pair_joined = lax.all_gather(own_joined, "tl", axis=0, tiled=False)
    pair_out = lax.all_gather(out_weight, "tl", axis=0, tiled=True)

    spread = jnp.broadcast_to(normed[None], (n_group,) + normed.shape)
    gathered = lax.all_to_all(spread, "th", 0, 0, tiled=True).reshape(group_rows, -1)
    width = own_joined.shape[1]
    mixed = jnp.dot(
        gathered,
        jnp.concatenate([pair_joined[c] for c in range(n_pair)], axis=1),
        preferred_element_type=jnp.float32,
    ).reshape(group_rows, n_pair, width)
    queries = mixed[:, :, :head_dim]
    full_key = mixed[:, :, head_dim : head_dim + half_kv].reshape(
        group_rows, kv_local, 2 * half_kv
    )
    full_value = mixed[:, :, head_dim + half_kv :].reshape(group_rows, kv_local, 2 * half_kv)

    member = jnp.arange(group_rows, dtype=jnp.int32) // local_rows
    within = jnp.arange(group_rows, dtype=jnp.int32) % local_rows
    row_ids = seq_index * seq_rows + (member * n_pair + pair_index) * local_rows + within
    row_segments = jnp.take(segment_ids, row_ids)
    positions = row_ids - segment_starts_of(row_segments, seg_lengths)

    q_rot = rotate(queries, positions).astype(jnp.bfloat16)
    k_rot = rotate(full_key, positions).astype(jnp.bfloat16)
    v_bf = full_value.astype(jnp.bfloat16)

    kv = jnp.concatenate([k_rot, v_bf], axis=2)
    kv_all = lax.all_gather(kv, ("seq", "tl"), axis=0, tiled=True)
    kv_all = kv_all.reshape(n_seq, n_pair, n_group, local_rows, kv_local, 2 * head_dim)
    kv_all = jnp.transpose(kv_all, (0, 2, 1, 3, 4, 5)).reshape(tokens, kv_local, 2 * head_dim)
    key_rows = kv_all[:, :, :head_dim]
    value_rows = kv_all[:, :, head_dim:]

    chunk_rows = group_rows // Q_CHUNKS
    member_part = local_rows // Q_CHUNKS
    q_chunks = jnp.transpose(
        q_rot.reshape(n_group, Q_CHUNKS, member_part, n_pair, head_dim), (1, 0, 2, 3, 4)
    ).reshape(Q_CHUNKS, chunk_rows, kv_local, 2, head_dim)
    q_ids = jnp.transpose(row_ids.reshape(n_group, Q_CHUNKS, member_part), (1, 0, 2)).reshape(
        Q_CHUNKS, chunk_rows
    )
    q_segs = jnp.transpose(
        row_segments.reshape(n_group, Q_CHUNKS, member_part), (1, 0, 2)
    ).reshape(Q_CHUNKS, chunk_rows)
    q_pos = jnp.transpose(positions.reshape(n_group, Q_CHUNKS, member_part), (1, 0, 2)).reshape(
        Q_CHUNKS, chunk_rows
    )

    def attend(chunk):
        def tile(tile_index, state):
            numer_one, denom_one = state
            k_start = tile_index * KEY_TILE
            k_block = lax.dynamic_slice_in_dim(key_rows, k_start, KEY_TILE, 0)
            v_block = lax.dynamic_slice_in_dim(value_rows, k_start, KEY_TILE, 0)
            k_segs = lax.dynamic_slice_in_dim(segment_ids, k_start, KEY_TILE, 0)
            k_ids = k_start + jnp.arange(KEY_TILE, dtype=jnp.int32)

            scores = (
                jnp.einsum(
                    "qkgd,tkd->kgqt",
                    q_chunks[chunk],
                    k_block,
                    preferred_element_type=jnp.float32,
                )
                * QUERY_SCALE
            )
            scores = SOFTCAP * jnp.tanh(scores / SOFTCAP)
            live = (k_ids[None, :] <= q_ids[chunk][:, None]) & (
                k_segs[None, :] == q_segs[chunk][:, None]
            )
            weights = jnp.where(live[None, None], jnp.exp(scores - SCORE_SHIFT), 0.0)
            denom_one = denom_one + jnp.sum(weights, axis=-1)
            numer_one = numer_one + jnp.einsum(
                "kgqt,tkd->qkgd",
                weights.astype(jnp.bfloat16),
                v_block,
                preferred_element_type=jnp.float32,
            )
            return (numer_one, denom_one)

        zero_numer = jnp.zeros((chunk_rows, kv_local, 2, head_dim), jnp.float32)
        zero_denom = jnp.zeros((kv_local, 2, chunk_rows), jnp.float32)
        lo_tile = jnp.min(q_ids[chunk] - q_pos[chunk]) // KEY_TILE
        hi_tile = jnp.max(q_ids[chunk]) // KEY_TILE + 1
        numer, denom = lax.fori_loop(lo_tile, hi_tile, tile, (zero_numer, zero_denom))
        denom_rows = jnp.transpose(denom, (2, 0, 1))[..., None]
        attended = (numer / denom_rows).astype(jnp.bfloat16).reshape(
            chunk_rows, n_pair * head_dim
        )
        partial = jnp.dot(attended, pair_out, preferred_element_type=jnp.float32).astype(
            jnp.bfloat16
        )
        pieces = lax.all_to_all(
            partial.reshape(n_group, member_part, -1), "th", 0, 0, tiled=True
        )
        return jnp.sum(pieces.astype(jnp.float32), axis=0)

    projected = jnp.concatenate([attend(chunk) for chunk in range(Q_CHUNKS)], axis=0)
    hidden_out = (hidden + rms_scale(projected, post_gain)).astype(jnp.bfloat16)

    cache_len = tokens // 2
    part_len = cache_len // n_seq
    request_ids = jnp.arange(slot_count, dtype=jnp.int32)
    starts = jnp.cumsum(seg_lengths) - seg_lengths
    own_offset = pair_index * half_kv
    own_keys = lax.dynamic_slice_in_dim(key_rows.reshape(tokens, -1), own_offset, half_kv, 1)
    own_values = lax.dynamic_slice_in_dim(
        value_rows.reshape(tokens, -1), own_offset, half_kv, 1
    )
    keys_pad = jnp.concatenate([own_keys, jnp.zeros((cache_len, half_kv), jnp.bfloat16)], 0)
    values_pad = jnp.concatenate(
        [own_values, jnp.zeros((cache_len, half_kv), jnp.bfloat16)], 0
    )
    seg_pad = jnp.concatenate([segment_ids, jnp.full((cache_len,), -1, jnp.int32)], 0)
    key_slots = []
    value_slots = []
    for slot_index in range(slot_count):
        request = jnp.sum(jnp.where(slot_map == slot_index, request_ids, 0)).astype(jnp.int32)
        first_row = jnp.sum(jnp.where(request_ids == request, starts, 0)).astype(jnp.int32)
        row0 = first_row + seq_index * part_len
        keep = (lax.dynamic_slice_in_dim(seg_pad, row0, part_len, 0) == request)[:, None]
        key_slots.append(
            jnp.where(
                keep,
                lax.dynamic_slice_in_dim(keys_pad, row0, part_len, 0),
                jnp.zeros((), jnp.bfloat16),
            )
        )
        value_slots.append(
            jnp.where(
                keep,
                lax.dynamic_slice_in_dim(values_pad, row0, part_len, 0),
                jnp.zeros((), jnp.bfloat16),
            )
        )
    return (hidden_out, jnp.stack(key_slots), jnp.stack(value_slots))


def solution(mesh):
    devices = np.asarray(mesh.devices)
    n_seq, n_tensor = devices.shape
    split = Mesh(
        devices.reshape(n_seq, n_tensor // HEADS_PER_DEVICE, HEADS_PER_DEVICE),
        ("seq", "th", "tl"),
    )
    rows = P(("seq", "th", "tl"), None)
    cols = P(None, ("th", "tl"))
    return jax.shard_map(
        on_device,
        mesh=split,
        in_specs=(
            rows,
            P(),
            cols,
            cols,
            cols,
            P(("th", "tl"), None),
            P(),
            P(),
            P(),
            P(),
        ),
        out_specs=(rows, P(None, "seq", ("th", "tl")), P(None, "seq", ("th", "tl"))),
        check_vma=False,
    )
```

```python
import jax
import jax.numpy as jnp
import numpy as np
from jax import lax
from jax.sharding import Mesh
from jax.sharding import PartitionSpec as P

HD = 128


EPSILON = 1e-06
SOFTCAP = 50.0
QUERY_SCALE = 144.0 ** (-0.5)
SCORE_SHIFT = 20.0
ROPE_BASE = 10000.0
KEY_TILE = 512
Q_CHUNKS = 2
HEADS_PER_DEVICE = 4


def rms_scale(values, gain):
    mean_sq = jnp.mean(values * values, axis=-1, keepdims=True)
    return values * lax.rsqrt(mean_sq + EPSILON) * gain


def rotate(values, positions):
    head_dim = values.shape[-1]
    half_dim = head_dim // 2
    freqs = ROPE_BASE ** (-2.0 * jnp.arange(half_dim, dtype=jnp.float32) / head_dim)
    angles = positions.astype(jnp.float32)[:, None] * freqs[None, :]
    cosine = jnp.cos(angles)[:, None, :]
    sine = jnp.sin(angles)[:, None, :]
    first = values[..., :half_dim]
    second = values[..., half_dim:]
    return jnp.concatenate(
        [first * cosine - second * sine, second * cosine + first * sine], axis=-1
    )


def segment_starts_of(row_segments, seg_lengths):
    starts = jnp.cumsum(seg_lengths) - seg_lengths
    request_ids = jnp.arange(seg_lengths.shape[0], dtype=jnp.int32)
    return jnp.sum(
        jnp.where(row_segments[:, None] == request_ids[None, :], starts[None, :], 0), axis=1
    )


def on_device(
    hidden_in,
    norm_gain,
    query_weight,
    key_weight,
    value_weight,
    out_weight,
    post_gain,
    seg_lengths,
    segment_ids,
    slot_map,
):
    n_group = lax.axis_size("th")
    n_seq = lax.axis_size("seq")
    n_pair = lax.axis_size("tl")
    kv_local = n_pair // 2
    local_rows = hidden_in.shape[0]
    tokens = segment_ids.shape[0]
    group_rows = local_rows * n_group
    seq_rows = group_rows * n_pair
    head_dim = HD
    half_kv = key_weight.shape[1]
    seq_index = lax.axis_index("seq")
    pair_index = lax.axis_index("tl")
    slot_count = seg_lengths.shape[0]

    hidden = hidden_in.astype(jnp.float32)
    normed = rms_scale(hidden, norm_gain).astype(jnp.bfloat16)

    own_joined = jnp.concatenate([query_weight, key_weight, value_weight], axis=1)
    pair_joined = lax.all_gather(own_joined, "tl", axis=0, tiled=False)
    pair_out = lax.all_gather(out_weight, "tl", axis=0, tiled=True)

    spread = jnp.broadcast_to(normed[None], (n_group,) + normed.shape)
    gathered = lax.all_to_all(spread, "th", 0, 0, tiled=True).reshape(group_rows, -1)
    width = own_joined.shape[1]
    mixed = jnp.einsum(
        "rd,cdw->rcw", gathered, pair_joined, preferred_element_type=jnp.float32
    )
    queries = mixed[:, :, :head_dim]
    full_key = mixed[:, :, head_dim : head_dim + half_kv].reshape(
        group_rows, kv_local, 2 * half_kv
    )
    full_value = mixed[:, :, head_dim + half_kv :].reshape(group_rows, kv_local, 2 * half_kv)

    member = jnp.arange(group_rows, dtype=jnp.int32) // local_rows
    within = jnp.arange(group_rows, dtype=jnp.int32) % local_rows
    row_ids = seq_index * seq_rows + (member * n_pair + pair_index) * local_rows + within
    row_segments = jnp.take(segment_ids, row_ids)
    positions = row_ids - segment_starts_of(row_segments, seg_lengths)

    q_rot = rotate(queries, positions).astype(jnp.bfloat16)
    k_rot = rotate(full_key, positions).astype(jnp.bfloat16)
    v_bf = full_value.astype(jnp.bfloat16)

    kv = jnp.concatenate([k_rot, v_bf], axis=2)
    kv_all = lax.all_gather(kv, ("seq", "tl"), axis=0, tiled=True)
    kv_all = kv_all.reshape(n_seq, n_pair, n_group, local_rows, kv_local, 2, head_dim)
    kv_all = jnp.transpose(kv_all, (5, 4, 0, 2, 1, 3, 6)).reshape(2, kv_local, tokens, head_dim)
    key_rows = kv_all[0]
    value_rows = kv_all[1]

    chunk_rows = group_rows // Q_CHUNKS
    member_part = local_rows // Q_CHUNKS
    q_chunks = jnp.transpose(
        q_rot.reshape(n_group, Q_CHUNKS, member_part, n_pair, head_dim), (1, 0, 2, 3, 4)
    ).reshape(Q_CHUNKS, chunk_rows, kv_local, 2, head_dim)
    q_ids = jnp.transpose(row_ids.reshape(n_group, Q_CHUNKS, member_part), (1, 0, 2)).reshape(
        Q_CHUNKS, chunk_rows
    )
    q_segs = jnp.transpose(
        row_segments.reshape(n_group, Q_CHUNKS, member_part), (1, 0, 2)
    ).reshape(Q_CHUNKS, chunk_rows)
    q_pos = jnp.transpose(positions.reshape(n_group, Q_CHUNKS, member_part), (1, 0, 2)).reshape(
        Q_CHUNKS, chunk_rows
    )

    def attend(chunk):
        def tile(tile_index, state):
            numer_one, denom_one = state
            k_start = tile_index * KEY_TILE
            k_block = lax.dynamic_slice_in_dim(key_rows, k_start, KEY_TILE, 1)
            v_block = lax.dynamic_slice_in_dim(value_rows, k_start, KEY_TILE, 1)
            k_segs = lax.dynamic_slice_in_dim(segment_ids, k_start, KEY_TILE, 0)
            k_ids = k_start + jnp.arange(KEY_TILE, dtype=jnp.int32)

            scores = (
                jnp.einsum(
                    "qkgd,ktd->kgqt",
                    q_chunks[chunk],
                    k_block,
                    preferred_element_type=jnp.float32,
                )
                * QUERY_SCALE
            )
            scores = SOFTCAP * jnp.tanh(scores / SOFTCAP)
            live = (k_ids[None, :] <= q_ids[chunk][:, None]) & (
                k_segs[None, :] == q_segs[chunk][:, None]
            )
            weights = jnp.where(live[None, None], jnp.exp(scores - SCORE_SHIFT), 0.0)
            denom_one = denom_one + jnp.sum(weights, axis=-1)
            numer_one = numer_one + jnp.einsum(
                "kgqt,ktd->qkgd",
                weights.astype(jnp.bfloat16),
                v_block,
                preferred_element_type=jnp.float32,
            )
            return (numer_one, denom_one)

        zero_numer = jnp.zeros((chunk_rows, kv_local, 2, head_dim), jnp.float32)
        zero_denom = jnp.zeros((kv_local, 2, chunk_rows), jnp.float32)
        lo_tile = jnp.min(q_ids[chunk] - q_pos[chunk]) // KEY_TILE
        hi_tile = jnp.max(q_ids[chunk]) // KEY_TILE + 1
        numer, denom = lax.fori_loop(lo_tile, hi_tile, tile, (zero_numer, zero_denom))
        denom_rows = jnp.transpose(denom, (2, 0, 1))[..., None]
        attended = (numer / denom_rows).astype(jnp.bfloat16).reshape(
            chunk_rows, n_pair * head_dim
        )
        partial = jnp.dot(attended, pair_out, preferred_element_type=jnp.float32).astype(
            jnp.bfloat16
        )
        pieces = lax.all_to_all(
            partial.reshape(n_group, member_part, -1), "th", 0, 0, tiled=True
        )
        return jnp.sum(pieces.astype(jnp.float32), axis=0)

    projected = jnp.concatenate([attend(chunk) for chunk in range(Q_CHUNKS)], axis=0)
    hidden_out = (hidden + rms_scale(projected, post_gain)).astype(jnp.bfloat16)

    cache_len = tokens // 2
    part_len = cache_len // n_seq
    request_ids = jnp.arange(slot_count, dtype=jnp.int32)
    starts = jnp.cumsum(seg_lengths) - seg_lengths
    own_head = pair_index // 2
    own_offset = pair_index % 2 * half_kv
    own_keys = lax.dynamic_slice_in_dim(
        lax.dynamic_index_in_dim(key_rows, own_head, 0, keepdims=False), own_offset, half_kv, 1
    )
    own_values = lax.dynamic_slice_in_dim(
        lax.dynamic_index_in_dim(value_rows, own_head, 0, keepdims=False), own_offset, half_kv, 1
    )
    keys_pad = jnp.concatenate([own_keys, jnp.zeros((cache_len, half_kv), jnp.bfloat16)], 0)
    values_pad = jnp.concatenate(
        [own_values, jnp.zeros((cache_len, half_kv), jnp.bfloat16)], 0
    )
    seg_pad = jnp.concatenate([segment_ids, jnp.full((cache_len,), -1, jnp.int32)], 0)
    key_slots = []
    value_slots = []
    for slot_index in range(slot_count):
        request = jnp.sum(jnp.where(slot_map == slot_index, request_ids, 0)).astype(jnp.int32)
        first_row = jnp.sum(jnp.where(request_ids == request, starts, 0)).astype(jnp.int32)
        row0 = first_row + seq_index * part_len
        keep = (lax.dynamic_slice_in_dim(seg_pad, row0, part_len, 0) == request)[:, None]
        key_slots.append(
            jnp.where(
                keep,
                lax.dynamic_slice_in_dim(keys_pad, row0, part_len, 0),
                jnp.zeros((), jnp.bfloat16),
            )
        )
        value_slots.append(
            jnp.where(
                keep,
                lax.dynamic_slice_in_dim(values_pad, row0, part_len, 0),
                jnp.zeros((), jnp.bfloat16),
            )
        )
    return (hidden_out, jnp.stack(key_slots), jnp.stack(value_slots))


def solution(mesh):
    devices = np.asarray(mesh.devices)
    n_seq, n_tensor = devices.shape
    split = Mesh(
        devices.reshape(n_seq, n_tensor // HEADS_PER_DEVICE, HEADS_PER_DEVICE),
        ("seq", "th", "tl"),
    )
    rows = P(("seq", "th", "tl"), None)
    cols = P(None, ("th", "tl"))
    return jax.shard_map(
        on_device,
        mesh=split,
        in_specs=(
            rows,
            P(),
            cols,
            cols,
            cols,
            P(("th", "tl"), None),
            P(),
            P(),
            P(),
            P(),
        ),
        out_specs=(rows, P(None, "seq", ("th", "tl")), P(None, "seq", ("th", "tl"))),
        check_vma=False,
    )
```

```python
import jax
import jax.numpy as jnp
import numpy as np
from jax import lax
from jax.sharding import Mesh
from jax.sharding import PartitionSpec as P

HD = 128


EPSILON = 1e-06
SOFTCAP = 50.0
QUERY_SCALE = 144.0 ** (-0.5)
SCORE_SHIFT = 20.0
ROPE_BASE = 10000.0
Q_CHUNKS = 2
HEADS_PER_DEVICE = 4


def rms_scale(values, gain):
    mean_sq = jnp.mean(values * values, axis=-1, keepdims=True)
    return values * lax.rsqrt(mean_sq + EPSILON) * gain


def rotate(values, positions):
    head_dim = values.shape[-1]
    half_dim = head_dim // 2
    freqs = ROPE_BASE ** (-2.0 * jnp.arange(half_dim, dtype=jnp.float32) / head_dim)
    angles = positions.astype(jnp.float32)[:, None] * freqs[None, :]
    cosine = jnp.cos(angles)[:, None, :]
    sine = jnp.sin(angles)[:, None, :]
    first = values[..., :half_dim]
    second = values[..., half_dim:]
    return jnp.concatenate(
        [first * cosine - second * sine, second * cosine + first * sine], axis=-1
    )


def segment_starts_of(row_segments, seg_lengths):
    starts = jnp.cumsum(seg_lengths) - seg_lengths
    request_ids = jnp.arange(seg_lengths.shape[0], dtype=jnp.int32)
    return jnp.sum(
        jnp.where(row_segments[:, None] == request_ids[None, :], starts[None, :], 0), axis=1
    )


def on_device(
    hidden_in,
    norm_gain,
    query_weight,
    key_weight,
    value_weight,
    out_weight,
    post_gain,
    seg_lengths,
    segment_ids,
    slot_map,
):
    n_group = lax.axis_size("th")
    n_seq = lax.axis_size("seq")
    n_pair = lax.axis_size("tl")
    kv_local = n_pair // 2
    local_rows = hidden_in.shape[0]
    tokens = segment_ids.shape[0]
    group_rows = local_rows * n_group
    seq_rows = group_rows * n_pair
    head_dim = HD
    half_kv = key_weight.shape[1]
    seq_index = lax.axis_index("seq")
    pair_index = lax.axis_index("tl")
    slot_count = seg_lengths.shape[0]

    hidden = hidden_in.astype(jnp.float32)
    normed = rms_scale(hidden, norm_gain).astype(jnp.bfloat16)

    own_joined = jnp.concatenate([query_weight, key_weight, value_weight], axis=1)
    pair_joined = lax.all_gather(own_joined, "tl", axis=0, tiled=False)
    pair_out = lax.all_gather(out_weight, "tl", axis=0, tiled=True)

    spread = jnp.broadcast_to(normed[None], (n_group,) + normed.shape)
    gathered = lax.all_to_all(spread, "th", 0, 0, tiled=True).reshape(group_rows, -1)
    width = own_joined.shape[1]
    mixed = jnp.einsum(
        "rd,cdw->rcw", gathered, pair_joined, preferred_element_type=jnp.float32
    )
    queries = mixed[:, :, :head_dim]
    full_key = mixed[:, :, head_dim : head_dim + half_kv].reshape(
        group_rows, kv_local, 2 * half_kv
    )
    full_value = mixed[:, :, head_dim + half_kv :].reshape(group_rows, kv_local, 2 * half_kv)

    member = jnp.arange(group_rows, dtype=jnp.int32) // local_rows
    within = jnp.arange(group_rows, dtype=jnp.int32) % local_rows
    row_ids = seq_index * seq_rows + (member * n_pair + pair_index) * local_rows + within
    row_segments = jnp.take(segment_ids, row_ids)
    positions = row_ids - segment_starts_of(row_segments, seg_lengths)

    q_rot = rotate(queries, positions).astype(jnp.bfloat16)
    k_rot = rotate(full_key, positions).astype(jnp.bfloat16)
    v_bf = full_value.astype(jnp.bfloat16)

    kv = jnp.stack([jnp.transpose(k_rot, (1, 0, 2)), jnp.transpose(v_bf, (1, 0, 2))])
    kv_all = lax.all_gather(kv, ("seq", "tl"), axis=2, tiled=True)
    key_rows = kv_all[0]
    value_rows = kv_all[1]
    gathered_index = jnp.arange(tokens, dtype=jnp.int32)
    block = gathered_index // group_rows
    in_block = gathered_index % group_rows
    perm_ids = (
        block // n_pair * seq_rows
        + ((in_block // local_rows) * n_pair + block % n_pair) * local_rows
        + in_block % local_rows
    )
    perm_segs = jnp.take(segment_ids, perm_ids)

    chunk_rows = group_rows // Q_CHUNKS
    member_part = local_rows // Q_CHUNKS
    q_chunks = jnp.transpose(
        q_rot.reshape(n_group, Q_CHUNKS, member_part, n_pair, head_dim), (1, 0, 2, 3, 4)
    ).reshape(Q_CHUNKS, chunk_rows, kv_local, 2, head_dim)
    q_ids = jnp.transpose(row_ids.reshape(n_group, Q_CHUNKS, member_part), (1, 0, 2)).reshape(
        Q_CHUNKS, chunk_rows
    )
    q_segs = jnp.transpose(
        row_segments.reshape(n_group, Q_CHUNKS, member_part), (1, 0, 2)
    ).reshape(Q_CHUNKS, chunk_rows)
    q_pos = jnp.transpose(positions.reshape(n_group, Q_CHUNKS, member_part), (1, 0, 2)).reshape(
        Q_CHUNKS, chunk_rows
    )

    def attend(chunk):
        def tile(tile_index, state):
            numer_one, denom_one = state
            k_start = tile_index * group_rows
            k_block = lax.dynamic_slice_in_dim(key_rows, k_start, group_rows, 1)
            v_block = lax.dynamic_slice_in_dim(value_rows, k_start, group_rows, 1)
            k_segs = lax.dynamic_slice_in_dim(perm_segs, k_start, group_rows, 0)
            k_ids = lax.dynamic_slice_in_dim(perm_ids, k_start, group_rows, 0)

            scores = (
                jnp.einsum(
                    "qkgd,ktd->kgqt",
                    q_chunks[chunk],
                    k_block,
                    preferred_element_type=jnp.float32,
                )
                * QUERY_SCALE
            )
            scores = SOFTCAP * jnp.tanh(scores / SOFTCAP)
            live = (k_ids[None, :] <= q_ids[chunk][:, None]) & (
                k_segs[None, :] == q_segs[chunk][:, None]
            )
            weights = jnp.where(live[None, None], jnp.exp(scores - SCORE_SHIFT), 0.0)
            denom_one = denom_one + jnp.sum(weights, axis=-1)
            numer_one = numer_one + jnp.einsum(
                "kgqt,ktd->qkgd",
                weights.astype(jnp.bfloat16),
                v_block,
                preferred_element_type=jnp.float32,
            )
            return (numer_one, denom_one)

        zero_numer = jnp.zeros((chunk_rows, kv_local, 2, head_dim), jnp.float32)
        zero_denom = jnp.zeros((kv_local, 2, chunk_rows), jnp.float32)
        lo_tile = jnp.min(q_ids[chunk] - q_pos[chunk]) // seq_rows * n_pair
        hi_tile = (seq_index + 1) * n_pair
        numer, denom = lax.fori_loop(lo_tile, hi_tile, tile, (zero_numer, zero_denom))
        denom_rows = jnp.transpose(denom, (2, 0, 1))[..., None]
        attended = (numer / denom_rows).astype(jnp.bfloat16).reshape(
            chunk_rows, n_pair * head_dim
        )
        partial = jnp.dot(attended, pair_out, preferred_element_type=jnp.float32).astype(
            jnp.bfloat16
        )
        pieces = lax.all_to_all(
            partial.reshape(n_group, member_part, -1), "th", 0, 0, tiled=True
        )
        return jnp.sum(pieces.astype(jnp.float32), axis=0)

    projected = jnp.concatenate([attend(chunk) for chunk in range(Q_CHUNKS)], axis=0)
    hidden_out = (hidden + rms_scale(projected, post_gain)).astype(jnp.bfloat16)

    cache_len = tokens // 2
    part_len = cache_len // n_seq
    request_ids = jnp.arange(slot_count, dtype=jnp.int32)
    starts = jnp.cumsum(seg_lengths) - seg_lengths
    own_head = pair_index // 2
    own_offset = pair_index % 2 * half_kv

    def stream_order(rows):
        own = lax.dynamic_slice_in_dim(
            lax.dynamic_index_in_dim(rows, own_head, 0, keepdims=False), own_offset, half_kv, 1
        )
        own = own.reshape(n_seq, n_pair, n_group, local_rows, half_kv)
        return jnp.transpose(own, (0, 2, 1, 3, 4)).reshape(tokens, half_kv)

    own_keys = stream_order(key_rows)
    own_values = stream_order(value_rows)
    keys_pad = jnp.concatenate([own_keys, jnp.zeros((cache_len, half_kv), jnp.bfloat16)], 0)
    values_pad = jnp.concatenate(
        [own_values, jnp.zeros((cache_len, half_kv), jnp.bfloat16)], 0
    )
    seg_pad = jnp.concatenate([segment_ids, jnp.full((cache_len,), -1, jnp.int32)], 0)
    key_slots = []
    value_slots = []
    for slot_index in range(slot_count):
        request = jnp.sum(jnp.where(slot_map == slot_index, request_ids, 0)).astype(jnp.int32)
        first_row = jnp.sum(jnp.where(request_ids == request, starts, 0)).astype(jnp.int32)
        row0 = first_row + seq_index * part_len
        keep = (lax.dynamic_slice_in_dim(seg_pad, row0, part_len, 0) == request)[:, None]
        key_slots.append(
            jnp.where(
                keep,
                lax.dynamic_slice_in_dim(keys_pad, row0, part_len, 0),
                jnp.zeros((), jnp.bfloat16),
            )
        )
        value_slots.append(
            jnp.where(
                keep,
                lax.dynamic_slice_in_dim(values_pad, row0, part_len, 0),
                jnp.zeros((), jnp.bfloat16),
            )
        )
    return (hidden_out, jnp.stack(key_slots), jnp.stack(value_slots))


def solution(mesh):
    devices = np.asarray(mesh.devices)
    n_seq, n_tensor = devices.shape
    split = Mesh(
        devices.reshape(n_seq, n_tensor // HEADS_PER_DEVICE, HEADS_PER_DEVICE),
        ("seq", "th", "tl"),
    )
    rows = P(("seq", "th", "tl"), None)
    cols = P(None, ("th", "tl"))
    return jax.shard_map(
        on_device,
        mesh=split,
        in_specs=(
            rows,
            P(),
            cols,
            cols,
            cols,
            P(("th", "tl"), None),
            P(),
            P(),
            P(),
            P(),
        ),
        out_specs=(rows, P(None, "seq", ("th", "tl")), P(None, "seq", ("th", "tl"))),
        check_vma=False,
    )
```

```python
import jax
import jax.numpy as jnp
import numpy as np
from jax import lax
from jax.sharding import Mesh
from jax.sharding import PartitionSpec as P

HD = 128


EPSILON = 1e-06
SOFTCAP = 50.0
QUERY_SCALE = 144.0 ** (-0.5)
SCORE_SHIFT = 20.0
ROPE_BASE = 10000.0
KEY_TILE = 512
Q_CHUNKS = 2
HEADS_PER_DEVICE = 4


def rms_scale(values, gain):
    mean_sq = jnp.mean(values * values, axis=-1, keepdims=True)
    return values * lax.rsqrt(mean_sq + EPSILON) * gain


def rotate(values, positions):
    head_dim = values.shape[-1]
    half_dim = head_dim // 2
    freqs = ROPE_BASE ** (-2.0 * jnp.arange(half_dim, dtype=jnp.float32) / head_dim)
    angles = positions.astype(jnp.float32)[:, None] * freqs[None, :]
    cosine = jnp.cos(angles)[:, None, :]
    sine = jnp.sin(angles)[:, None, :]
    first = values[..., :half_dim]
    second = values[..., half_dim:]
    return jnp.concatenate(
        [first * cosine - second * sine, second * cosine + first * sine], axis=-1
    )


def segment_starts_of(row_segments, seg_lengths):
    starts = jnp.cumsum(seg_lengths) - seg_lengths
    request_ids = jnp.arange(seg_lengths.shape[0], dtype=jnp.int32)
    return jnp.sum(
        jnp.where(row_segments[:, None] == request_ids[None, :], starts[None, :], 0), axis=1
    )


def on_device(
    hidden_in,
    norm_gain,
    query_weight,
    key_weight,
    value_weight,
    out_weight,
    post_gain,
    seg_lengths,
    segment_ids,
    slot_map,
):
    n_group = lax.axis_size("th")
    n_seq = lax.axis_size("seq")
    n_pair = lax.axis_size("tl")
    kv_local = n_pair // 2
    local_rows = hidden_in.shape[0]
    tokens = segment_ids.shape[0]
    group_rows = local_rows * n_group
    seq_rows = group_rows * n_pair
    head_dim = HD
    half_kv = key_weight.shape[1]
    seq_index = lax.axis_index("seq")
    pair_index = lax.axis_index("tl")
    slot_count = seg_lengths.shape[0]

    hidden = hidden_in.astype(jnp.float32)
    normed = rms_scale(hidden, norm_gain).astype(jnp.bfloat16)

    own_joined = jnp.concatenate([query_weight, key_weight, value_weight], axis=1)
    core = seq_index % 2
    fetched = lax.all_gather(
        jnp.where(core == 0, query_weight, jnp.concatenate([key_weight, value_weight], 1)),
        "tl",
        axis=0,
        tiled=False,
    )
    swapped = lax.ppermute(fetched, "seq", [(i, i ^ 1) for i in range(n_seq)])
    pair_out = lax.all_gather(out_weight, "tl", axis=0, tiled=True)

    spread = jnp.broadcast_to(normed[None], (n_group,) + normed.shape)
    gathered = lax.all_to_all(spread, "th", 0, 0, tiled=True).reshape(group_rows, -1)
    width = own_joined.shape[1]
    mixed_fetched = jnp.einsum(
        "rd,cdw->rcw", gathered, fetched, preferred_element_type=jnp.float32
    )
    mixed_swapped = jnp.einsum(
        "rd,cdw->rcw", gathered, swapped, preferred_element_type=jnp.float32
    )
    mixed = jnp.where(
        core == 0,
        jnp.concatenate([mixed_fetched, mixed_swapped], 2),
        jnp.concatenate([mixed_swapped, mixed_fetched], 2),
    )
    queries = mixed[:, :, :head_dim]
    full_key = mixed[:, :, head_dim : head_dim + half_kv].reshape(
        group_rows, kv_local, 2 * half_kv
    )
    full_value = mixed[:, :, head_dim + half_kv :].reshape(group_rows, kv_local, 2 * half_kv)

    member = jnp.arange(group_rows, dtype=jnp.int32) // local_rows
    within = jnp.arange(group_rows, dtype=jnp.int32) % local_rows
    row_ids = seq_index * seq_rows + (member * n_pair + pair_index) * local_rows + within
    row_segments = jnp.take(segment_ids, row_ids)
    positions = row_ids - segment_starts_of(row_segments, seg_lengths)

    q_rot = rotate(queries, positions).astype(jnp.bfloat16)
    k_rot = rotate(full_key, positions).astype(jnp.bfloat16)
    v_bf = full_value.astype(jnp.bfloat16)

    kv = jnp.concatenate([k_rot, v_bf], axis=2)
    kv_all = lax.all_gather(kv, ("seq", "tl"), axis=0, tiled=True)
    kv_all = kv_all.reshape(n_seq, n_pair, n_group, local_rows, kv_local, 2, head_dim)
    kv_all = jnp.transpose(kv_all, (5, 4, 0, 2, 1, 3, 6)).reshape(2, kv_local, tokens, head_dim)
    key_rows = kv_all[0]
    value_rows = kv_all[1]

    chunk_rows = group_rows // Q_CHUNKS
    member_part = local_rows // Q_CHUNKS
    q_chunks = jnp.transpose(
        q_rot.reshape(n_group, Q_CHUNKS, member_part, n_pair, head_dim), (1, 0, 2, 3, 4)
    ).reshape(Q_CHUNKS, chunk_rows, kv_local, 2, head_dim)
    q_ids = jnp.transpose(row_ids.reshape(n_group, Q_CHUNKS, member_part), (1, 0, 2)).reshape(
        Q_CHUNKS, chunk_rows
    )
    q_segs = jnp.transpose(
        row_segments.reshape(n_group, Q_CHUNKS, member_part), (1, 0, 2)
    ).reshape(Q_CHUNKS, chunk_rows)
    q_pos = jnp.transpose(positions.reshape(n_group, Q_CHUNKS, member_part), (1, 0, 2)).reshape(
        Q_CHUNKS, chunk_rows
    )

    def attend(chunk):
        def tile(tile_index, state):
            numer_one, denom_one = state
            k_start = tile_index * KEY_TILE
            k_block = lax.dynamic_slice_in_dim(key_rows, k_start, KEY_TILE, 1)
            v_block = lax.dynamic_slice_in_dim(value_rows, k_start, KEY_TILE, 1)
            k_segs = lax.dynamic_slice_in_dim(segment_ids, k_start, KEY_TILE, 0)
            k_ids = k_start + jnp.arange(KEY_TILE, dtype=jnp.int32)

            scores = (
                jnp.einsum(
                    "qkgd,ktd->kgqt",
                    q_chunks[chunk],
                    k_block,
                    preferred_element_type=jnp.float32,
                )
                * QUERY_SCALE
            )
            scores = SOFTCAP * jnp.tanh(scores / SOFTCAP)
            live = (k_ids[None, :] <= q_ids[chunk][:, None]) & (
                k_segs[None, :] == q_segs[chunk][:, None]
            )
            weights = jnp.where(live[None, None], jnp.exp(scores - SCORE_SHIFT), 0.0)
            denom_one = denom_one + jnp.sum(weights, axis=-1)
            numer_one = numer_one + jnp.einsum(
                "kgqt,ktd->qkgd",
                weights.astype(jnp.bfloat16),
                v_block,
                preferred_element_type=jnp.float32,
            )
            return (numer_one, denom_one)

        zero_numer = jnp.zeros((chunk_rows, kv_local, 2, head_dim), jnp.float32)
        zero_denom = jnp.zeros((kv_local, 2, chunk_rows), jnp.float32)
        lo_tile = jnp.min(q_ids[chunk] - q_pos[chunk]) // KEY_TILE
        hi_tile = jnp.max(q_ids[chunk]) // KEY_TILE + 1
        numer, denom = lax.fori_loop(lo_tile, hi_tile, tile, (zero_numer, zero_denom))
        denom_rows = jnp.transpose(denom, (2, 0, 1))[..., None]
        attended = (numer / denom_rows).astype(jnp.bfloat16).reshape(
            chunk_rows, n_pair * head_dim
        )
        partial = jnp.dot(attended, pair_out, preferred_element_type=jnp.float32).astype(
            jnp.bfloat16
        )
        pieces = lax.all_to_all(
            partial.reshape(n_group, member_part, -1), "th", 0, 0, tiled=True
        )
        return jnp.sum(pieces.astype(jnp.float32), axis=0)

    projected = jnp.concatenate([attend(chunk) for chunk in range(Q_CHUNKS)], axis=0)
    hidden_out = (hidden + rms_scale(projected, post_gain)).astype(jnp.bfloat16)

    cache_len = tokens // 2
    part_len = cache_len // n_seq
    request_ids = jnp.arange(slot_count, dtype=jnp.int32)
    starts = jnp.cumsum(seg_lengths) - seg_lengths
    own_head = pair_index // 2
    own_offset = pair_index % 2 * half_kv
    own_keys = lax.dynamic_slice_in_dim(
        lax.dynamic_index_in_dim(key_rows, own_head, 0, keepdims=False), own_offset, half_kv, 1
    )
    own_values = lax.dynamic_slice_in_dim(
        lax.dynamic_index_in_dim(value_rows, own_head, 0, keepdims=False), own_offset, half_kv, 1
    )
    keys_pad = jnp.concatenate([own_keys, jnp.zeros((cache_len, half_kv), jnp.bfloat16)], 0)
    values_pad = jnp.concatenate(
        [own_values, jnp.zeros((cache_len, half_kv), jnp.bfloat16)], 0
    )
    seg_pad = jnp.concatenate([segment_ids, jnp.full((cache_len,), -1, jnp.int32)], 0)
    key_slots = []
    value_slots = []
    for slot_index in range(slot_count):
        request = jnp.sum(jnp.where(slot_map == slot_index, request_ids, 0)).astype(jnp.int32)
        first_row = jnp.sum(jnp.where(request_ids == request, starts, 0)).astype(jnp.int32)
        row0 = first_row + seq_index * part_len
        keep = (lax.dynamic_slice_in_dim(seg_pad, row0, part_len, 0) == request)[:, None]
        key_slots.append(
            jnp.where(
                keep,
                lax.dynamic_slice_in_dim(keys_pad, row0, part_len, 0),
                jnp.zeros((), jnp.bfloat16),
            )
        )
        value_slots.append(
            jnp.where(
                keep,
                lax.dynamic_slice_in_dim(values_pad, row0, part_len, 0),
                jnp.zeros((), jnp.bfloat16),
            )
        )
    return (hidden_out, jnp.stack(key_slots), jnp.stack(value_slots))


def solution(mesh):
    devices = np.asarray(mesh.devices)
    n_seq, n_tensor = devices.shape
    split = Mesh(
        devices.reshape(n_seq, n_tensor // HEADS_PER_DEVICE, HEADS_PER_DEVICE),
        ("seq", "th", "tl"),
    )
    rows = P(("seq", "th", "tl"), None)
    cols = P(None, ("th", "tl"))
    return jax.shard_map(
        on_device,
        mesh=split,
        in_specs=(
            rows,
            P(),
            cols,
            cols,
            cols,
            P(("th", "tl"), None),
            P(),
            P(),
            P(),
            P(),
        ),
        out_specs=(rows, P(None, "seq", ("th", "tl")), P(None, "seq", ("th", "tl"))),
        check_vma=False,
    )
```

```python
import jax
import jax.numpy as jnp
import numpy as np
from jax import lax
from jax.sharding import Mesh
from jax.sharding import PartitionSpec as P

HD = 128


EPSILON = 1e-06
SOFTCAP = 50.0
QUERY_SCALE = 144.0 ** (-0.5)
SCORE_SHIFT = 20.0
ROPE_BASE = 10000.0
KEY_TILE = 512
Q_CHUNKS = 2
HEADS_PER_DEVICE = 4


def rms_scale(values, gain):
    mean_sq = jnp.mean(values * values, axis=-1, keepdims=True)
    return values * lax.rsqrt(mean_sq + EPSILON) * gain


def rotate(values, positions):
    head_dim = values.shape[-1]
    half_dim = head_dim // 2
    freqs = ROPE_BASE ** (-2.0 * jnp.arange(half_dim, dtype=jnp.float32) / head_dim)
    angles = positions.astype(jnp.float32)[:, None] * freqs[None, :]
    cosine = jnp.cos(angles)[:, None, :]
    sine = jnp.sin(angles)[:, None, :]
    first = values[..., :half_dim]
    second = values[..., half_dim:]
    return jnp.concatenate(
        [first * cosine - second * sine, second * cosine + first * sine], axis=-1
    )


def segment_starts_of(row_segments, seg_lengths):
    starts = jnp.cumsum(seg_lengths) - seg_lengths
    request_ids = jnp.arange(seg_lengths.shape[0], dtype=jnp.int32)
    return jnp.sum(
        jnp.where(row_segments[:, None] == request_ids[None, :], starts[None, :], 0), axis=1
    )


def on_device(
    hidden_in,
    norm_gain,
    query_weight,
    key_weight,
    value_weight,
    out_weight,
    post_gain,
    seg_lengths,
    segment_ids,
    slot_map,
):
    n_group = lax.axis_size("th")
    n_seq = lax.axis_size("seq")
    n_pair = lax.axis_size("tl")
    kv_local = n_pair // 2
    local_rows = hidden_in.shape[0]
    tokens = segment_ids.shape[0]
    group_rows = local_rows * n_group
    seq_rows = group_rows * n_pair
    head_dim = HD
    half_kv = key_weight.shape[1]
    seq_index = lax.axis_index("seq")
    pair_index = lax.axis_index("tl")
    slot_count = seg_lengths.shape[0]

    hidden = hidden_in.astype(jnp.float32)
    normed = rms_scale(hidden, norm_gain).astype(jnp.bfloat16)

    own_joined = jnp.concatenate([query_weight, key_weight, value_weight], axis=1)
    core = seq_index % 2
    fetched = lax.all_gather(
        jnp.where(core == 0, query_weight, jnp.concatenate([key_weight, value_weight], 1)),
        "tl",
        axis=0,
        tiled=False,
    )
    swapped = lax.ppermute(fetched, "seq", [(i, i ^ 1) for i in range(n_seq)])
    pair_out = lax.all_gather(out_weight, "tl", axis=0, tiled=True)

    spread = jnp.broadcast_to(normed[None], (n_group,) + normed.shape)
    gathered = lax.all_to_all(spread, "th", 0, 0, tiled=True).reshape(group_rows, -1)
    width = own_joined.shape[1]
    mixed_fetched = jnp.einsum(
        "rd,cdw->rcw", gathered, fetched, preferred_element_type=jnp.float32
    )
    mixed_swapped = jnp.einsum(
        "rd,cdw->rcw", gathered, swapped, preferred_element_type=jnp.float32
    )
    mixed = jnp.where(
        core == 0,
        jnp.concatenate([mixed_fetched, mixed_swapped], 2),
        jnp.concatenate([mixed_swapped, mixed_fetched], 2),
    )
    queries = mixed[:, :, :head_dim]
    full_key = mixed[:, :, head_dim : head_dim + half_kv].reshape(
        group_rows, kv_local, 2 * half_kv
    )
    full_value = mixed[:, :, head_dim + half_kv :].reshape(group_rows, kv_local, 2 * half_kv)

    member = jnp.arange(group_rows, dtype=jnp.int32) // local_rows
    within = jnp.arange(group_rows, dtype=jnp.int32) % local_rows
    row_ids = seq_index * seq_rows + (member * n_pair + pair_index) * local_rows + within
    row_segments = jnp.take(segment_ids, row_ids)
    positions = row_ids - segment_starts_of(row_segments, seg_lengths)

    q_rot = rotate(queries, positions).astype(jnp.bfloat16)
    k_rot = rotate(full_key, positions).astype(jnp.bfloat16)
    v_bf = full_value.astype(jnp.bfloat16)

    kv = jnp.stack([jnp.transpose(k_rot, (1, 0, 2)), jnp.transpose(v_bf, (1, 0, 2))])
    kv_all = lax.all_gather(kv, ("seq", "tl"), axis=2, tiled=True)
    kv_all = kv_all.reshape(2, kv_local, n_seq, n_pair, n_group, local_rows, head_dim)
    kv_all = jnp.transpose(kv_all, (0, 1, 2, 4, 3, 5, 6)).reshape(2, kv_local, tokens, head_dim)
    key_rows = kv_all[0]
    value_rows = kv_all[1]

    chunk_rows = group_rows // Q_CHUNKS
    member_part = local_rows // Q_CHUNKS
    q_chunks = jnp.transpose(
        q_rot.reshape(n_group, Q_CHUNKS, member_part, n_pair, head_dim), (1, 0, 2, 3, 4)
    ).reshape(Q_CHUNKS, chunk_rows, kv_local, 2, head_dim)
    q_ids = jnp.transpose(row_ids.reshape(n_group, Q_CHUNKS, member_part), (1, 0, 2)).reshape(
        Q_CHUNKS, chunk_rows
    )
    q_segs = jnp.transpose(
        row_segments.reshape(n_group, Q_CHUNKS, member_part), (1, 0, 2)
    ).reshape(Q_CHUNKS, chunk_rows)
    q_pos = jnp.transpose(positions.reshape(n_group, Q_CHUNKS, member_part), (1, 0, 2)).reshape(
        Q_CHUNKS, chunk_rows
    )

    def attend(chunk):
        def tile(tile_index, state):
            numer_one, denom_one = state
            k_start = tile_index * KEY_TILE
            k_block = lax.dynamic_slice_in_dim(key_rows, k_start, KEY_TILE, 1)
            v_block = lax.dynamic_slice_in_dim(value_rows, k_start, KEY_TILE, 1)
            k_segs = lax.dynamic_slice_in_dim(segment_ids, k_start, KEY_TILE, 0)
            k_ids = k_start + jnp.arange(KEY_TILE, dtype=jnp.int32)

            scores = (
                jnp.einsum(
                    "qkgd,ktd->kgqt",
                    q_chunks[chunk],
                    k_block,
                    preferred_element_type=jnp.float32,
                )
                * QUERY_SCALE
            )
            scores = SOFTCAP * jnp.tanh(scores / SOFTCAP)
            live = (k_ids[None, :] <= q_ids[chunk][:, None]) & (
                k_segs[None, :] == q_segs[chunk][:, None]
            )
            weights = jnp.where(live[None, None], jnp.exp(scores - SCORE_SHIFT), 0.0)
            denom_one = denom_one + jnp.sum(weights, axis=-1)
            numer_one = numer_one + jnp.einsum(
                "kgqt,ktd->qkgd",
                weights.astype(jnp.bfloat16),
                v_block,
                preferred_element_type=jnp.float32,
            )
            return (numer_one, denom_one)

        zero_numer = jnp.zeros((chunk_rows, kv_local, 2, head_dim), jnp.float32)
        zero_denom = jnp.zeros((kv_local, 2, chunk_rows), jnp.float32)
        lo_tile = jnp.min(q_ids[chunk] - q_pos[chunk]) // KEY_TILE
        hi_tile = jnp.max(q_ids[chunk]) // KEY_TILE + 1
        numer, denom = lax.fori_loop(lo_tile, hi_tile, tile, (zero_numer, zero_denom))
        denom_rows = jnp.transpose(denom, (2, 0, 1))[..., None]
        attended = (numer / denom_rows).astype(jnp.bfloat16).reshape(
            chunk_rows, n_pair * head_dim
        )
        partial = jnp.dot(attended, pair_out, preferred_element_type=jnp.float32).astype(
            jnp.bfloat16
        )
        pieces = lax.all_to_all(
            partial.reshape(n_group, member_part, -1), "th", 0, 0, tiled=True
        )
        return jnp.sum(pieces.astype(jnp.float32), axis=0)

    projected = jnp.concatenate([attend(chunk) for chunk in range(Q_CHUNKS)], axis=0)
    hidden_out = (hidden + rms_scale(projected, post_gain)).astype(jnp.bfloat16)

    cache_len = tokens // 2
    part_len = cache_len // n_seq
    request_ids = jnp.arange(slot_count, dtype=jnp.int32)
    starts = jnp.cumsum(seg_lengths) - seg_lengths
    own_head = pair_index // 2
    own_offset = pair_index % 2 * half_kv
    own_keys = lax.dynamic_slice_in_dim(
        lax.dynamic_index_in_dim(key_rows, own_head, 0, keepdims=False), own_offset, half_kv, 1
    )
    own_values = lax.dynamic_slice_in_dim(
        lax.dynamic_index_in_dim(value_rows, own_head, 0, keepdims=False), own_offset, half_kv, 1
    )
    keys_pad = jnp.concatenate([own_keys, jnp.zeros((cache_len, half_kv), jnp.bfloat16)], 0)
    values_pad = jnp.concatenate(
        [own_values, jnp.zeros((cache_len, half_kv), jnp.bfloat16)], 0
    )
    seg_pad = jnp.concatenate([segment_ids, jnp.full((cache_len,), -1, jnp.int32)], 0)
    key_slots = []
    value_slots = []
    for slot_index in range(slot_count):
        request = jnp.sum(jnp.where(slot_map == slot_index, request_ids, 0)).astype(jnp.int32)
        first_row = jnp.sum(jnp.where(request_ids == request, starts, 0)).astype(jnp.int32)
        row0 = first_row + seq_index * part_len
        keep = (lax.dynamic_slice_in_dim(seg_pad, row0, part_len, 0) == request)[:, None]
        key_slots.append(
            jnp.where(
                keep,
                lax.dynamic_slice_in_dim(keys_pad, row0, part_len, 0),
                jnp.zeros((), jnp.bfloat16),
            )
        )
        value_slots.append(
            jnp.where(
                keep,
                lax.dynamic_slice_in_dim(values_pad, row0, part_len, 0),
                jnp.zeros((), jnp.bfloat16),
            )
        )
    return (hidden_out, jnp.stack(key_slots), jnp.stack(value_slots))


def solution(mesh):
    devices = np.asarray(mesh.devices)
    n_seq, n_tensor = devices.shape
    split = Mesh(
        devices.reshape(n_seq, n_tensor // HEADS_PER_DEVICE, HEADS_PER_DEVICE),
        ("seq", "th", "tl"),
    )
    rows = P(("seq", "th", "tl"), None)
    cols = P(None, ("th", "tl"))
    return jax.shard_map(
        on_device,
        mesh=split,
        in_specs=(
            rows,
            P(),
            cols,
            cols,
            cols,
            P(("th", "tl"), None),
            P(),
            P(),
            P(),
            P(),
        ),
        out_specs=(rows, P(None, "seq", ("th", "tl")), P(None, "seq", ("th", "tl"))),
        check_vma=False,
    )
```

```python
import jax
import jax.numpy as jnp
import numpy as np
from jax import lax
from jax.sharding import Mesh
from jax.sharding import PartitionSpec as P

HD = 128


EPSILON = 1e-06
SOFTCAP = 50.0
QUERY_SCALE = 144.0 ** (-0.5)
SCORE_SHIFT = 20.0
ROPE_BASE = 10000.0
KEY_TILE = 512
Q_CHUNKS = 2
HEADS_PER_DEVICE = 4


def rms_scale(values, gain):
    mean_sq = jnp.mean(values * values, axis=-1, keepdims=True)
    return values * lax.rsqrt(mean_sq + EPSILON) * gain


def rotate(values, positions):
    head_dim = values.shape[-1]
    half_dim = head_dim // 2
    freqs = ROPE_BASE ** (-2.0 * jnp.arange(half_dim, dtype=jnp.float32) / head_dim)
    angles = positions.astype(jnp.float32)[:, None] * freqs[None, :]
    cosine = jnp.cos(angles)[:, None, :]
    sine = jnp.sin(angles)[:, None, :]
    first = values[..., :half_dim]
    second = values[..., half_dim:]
    return jnp.concatenate(
        [first * cosine - second * sine, second * cosine + first * sine], axis=-1
    )


def segment_starts_of(row_segments, seg_lengths):
    starts = jnp.cumsum(seg_lengths) - seg_lengths
    request_ids = jnp.arange(seg_lengths.shape[0], dtype=jnp.int32)
    return jnp.sum(
        jnp.where(row_segments[:, None] == request_ids[None, :], starts[None, :], 0), axis=1
    )


def on_device(
    hidden_in,
    norm_gain,
    query_weight,
    key_weight,
    value_weight,
    out_weight,
    post_gain,
    seg_lengths,
    segment_ids,
    slot_map,
):
    n_group = lax.axis_size("th")
    n_seq = lax.axis_size("sh") * lax.axis_size("core")
    n_pair = lax.axis_size("tl")
    kv_local = n_pair // 2
    local_rows = hidden_in.shape[0]
    tokens = segment_ids.shape[0]
    group_rows = local_rows * n_group
    seq_rows = group_rows * n_pair
    head_dim = HD
    half_kv = key_weight.shape[1]
    core = lax.axis_index("core")
    seq_index = lax.axis_index("sh") * lax.axis_size("core") + core
    pair_index = lax.axis_index("tl")
    slot_count = seg_lengths.shape[0]

    hidden = hidden_in.astype(jnp.float32)
    normed = rms_scale(hidden, norm_gain).astype(jnp.bfloat16)

    own_joined = jnp.concatenate([query_weight, key_weight, value_weight], axis=1)
    fetched = lax.all_gather(
        jnp.where(core == 0, query_weight, jnp.concatenate([key_weight, value_weight], 1)),
        "tl",
        axis=0,
        tiled=False,
    )
    swapped = lax.ppermute(fetched, "core", [(0, 1), (1, 0)])
    pair_out = lax.all_gather(out_weight, "tl", axis=0, tiled=True)

    spread = jnp.broadcast_to(normed[None], (n_group,) + normed.shape)
    gathered = lax.all_to_all(spread, "th", 0, 0, tiled=True).reshape(group_rows, -1)
    width = own_joined.shape[1]
    mixed_fetched = jnp.einsum(
        "rd,cdw->rcw", gathered, fetched, preferred_element_type=jnp.float32
    )
    mixed_swapped = jnp.einsum(
        "rd,cdw->rcw", gathered, swapped, preferred_element_type=jnp.float32
    )
    mixed = jnp.where(
        core == 0,
        jnp.concatenate([mixed_fetched, mixed_swapped], 2),
        jnp.concatenate([mixed_swapped, mixed_fetched], 2),
    )
    queries = mixed[:, :, :head_dim]
    full_key = mixed[:, :, head_dim : head_dim + half_kv].reshape(
        group_rows, kv_local, 2 * half_kv
    )
    full_value = mixed[:, :, head_dim + half_kv :].reshape(group_rows, kv_local, 2 * half_kv)

    member = jnp.arange(group_rows, dtype=jnp.int32) // local_rows
    within = jnp.arange(group_rows, dtype=jnp.int32) % local_rows
    row_ids = seq_index * seq_rows + (member * n_pair + pair_index) * local_rows + within
    row_segments = jnp.take(segment_ids, row_ids)
    positions = row_ids - segment_starts_of(row_segments, seg_lengths)

    q_rot = rotate(queries, positions).astype(jnp.bfloat16)
    k_rot = rotate(full_key, positions).astype(jnp.bfloat16)
    v_bf = full_value.astype(jnp.bfloat16)

    kv = jnp.stack([jnp.transpose(k_rot, (1, 0, 2)), jnp.transpose(v_bf, (1, 0, 2))])
    mine = lax.all_gather(kv, ("sh", "tl"), axis=2, tiled=True)
    theirs = lax.ppermute(mine, "core", [(0, 1), (1, 0)])
    n_sh = n_seq // 2
    mine = mine.reshape(2, kv_local, n_sh, 1, n_pair, n_group, local_rows, head_dim)
    theirs = theirs.reshape(2, kv_local, n_sh, 1, n_pair, n_group, local_rows, head_dim)
    kv_all = jnp.where(
        core == 0,
        jnp.concatenate([mine, theirs], axis=3),
        jnp.concatenate([theirs, mine], axis=3),
    )
    kv_all = jnp.transpose(kv_all, (0, 1, 2, 3, 5, 4, 6, 7)).reshape(
        2, kv_local, tokens, head_dim
    )
    key_rows = kv_all[0]
    value_rows = kv_all[1]

    chunk_rows = group_rows // Q_CHUNKS
    member_part = local_rows // Q_CHUNKS
    q_chunks = jnp.transpose(
        q_rot.reshape(n_group, Q_CHUNKS, member_part, n_pair, head_dim), (1, 0, 2, 3, 4)
    ).reshape(Q_CHUNKS, chunk_rows, kv_local, 2, head_dim)
    q_ids = jnp.transpose(row_ids.reshape(n_group, Q_CHUNKS, member_part), (1, 0, 2)).reshape(
        Q_CHUNKS, chunk_rows
    )
    q_segs = jnp.transpose(
        row_segments.reshape(n_group, Q_CHUNKS, member_part), (1, 0, 2)
    ).reshape(Q_CHUNKS, chunk_rows)
    q_pos = jnp.transpose(positions.reshape(n_group, Q_CHUNKS, member_part), (1, 0, 2)).reshape(
        Q_CHUNKS, chunk_rows
    )

    def attend(chunk):
        def tile(tile_index, state):
            numer_one, denom_one = state
            k_start = tile_index * KEY_TILE
            k_block = lax.dynamic_slice_in_dim(key_rows, k_start, KEY_TILE, 1)
            v_block = lax.dynamic_slice_in_dim(value_rows, k_start, KEY_TILE, 1)
            k_segs = lax.dynamic_slice_in_dim(segment_ids, k_start, KEY_TILE, 0)
            k_ids = k_start + jnp.arange(KEY_TILE, dtype=jnp.int32)

            scores = (
                jnp.einsum(
                    "qkgd,ktd->kgqt",
                    q_chunks[chunk],
                    k_block,
                    preferred_element_type=jnp.float32,
                )
                * QUERY_SCALE
            )
            scores = SOFTCAP * jnp.tanh(scores / SOFTCAP)
            live = (k_ids[None, :] <= q_ids[chunk][:, None]) & (
                k_segs[None, :] == q_segs[chunk][:, None]
            )
            weights = jnp.where(live[None, None], jnp.exp(scores - SCORE_SHIFT), 0.0)
            denom_one = denom_one + jnp.sum(weights, axis=-1)
            numer_one = numer_one + jnp.einsum(
                "kgqt,ktd->qkgd",
                weights.astype(jnp.bfloat16),
                v_block,
                preferred_element_type=jnp.float32,
            )
            return (numer_one, denom_one)

        zero_numer = jnp.zeros((chunk_rows, kv_local, 2, head_dim), jnp.float32)
        zero_denom = jnp.zeros((kv_local, 2, chunk_rows), jnp.float32)
        lo_tile = jnp.min(q_ids[chunk] - q_pos[chunk]) // KEY_TILE
        hi_tile = jnp.max(q_ids[chunk]) // KEY_TILE + 1
        numer, denom = lax.fori_loop(lo_tile, hi_tile, tile, (zero_numer, zero_denom))
        denom_rows = jnp.transpose(denom, (2, 0, 1))[..., None]
        attended = (numer / denom_rows).astype(jnp.bfloat16).reshape(
            chunk_rows, n_pair * head_dim
        )
        partial = jnp.dot(attended, pair_out, preferred_element_type=jnp.float32).astype(
            jnp.bfloat16
        )
        pieces = lax.all_to_all(
            partial.reshape(n_group, member_part, -1), "th", 0, 0, tiled=True
        )
        return jnp.sum(pieces.astype(jnp.float32), axis=0)

    projected = jnp.concatenate([attend(chunk) for chunk in range(Q_CHUNKS)], axis=0)
    hidden_out = (hidden + rms_scale(projected, post_gain)).astype(jnp.bfloat16)

    cache_len = tokens // 2
    part_len = cache_len // n_seq
    request_ids = jnp.arange(slot_count, dtype=jnp.int32)
    starts = jnp.cumsum(seg_lengths) - seg_lengths
    own_head = pair_index // 2
    own_offset = pair_index % 2 * half_kv
    own_keys = lax.dynamic_slice_in_dim(
        lax.dynamic_index_in_dim(key_rows, own_head, 0, keepdims=False), own_offset, half_kv, 1
    )
    own_values = lax.dynamic_slice_in_dim(
        lax.dynamic_index_in_dim(value_rows, own_head, 0, keepdims=False), own_offset, half_kv, 1
    )
    keys_pad = jnp.concatenate([own_keys, jnp.zeros((cache_len, half_kv), jnp.bfloat16)], 0)
    values_pad = jnp.concatenate(
        [own_values, jnp.zeros((cache_len, half_kv), jnp.bfloat16)], 0
    )
    seg_pad = jnp.concatenate([segment_ids, jnp.full((cache_len,), -1, jnp.int32)], 0)
    key_slots = []
    value_slots = []
    for slot_index in range(slot_count):
        request = jnp.sum(jnp.where(slot_map == slot_index, request_ids, 0)).astype(jnp.int32)
        first_row = jnp.sum(jnp.where(request_ids == request, starts, 0)).astype(jnp.int32)
        row0 = first_row + seq_index * part_len
        keep = (lax.dynamic_slice_in_dim(seg_pad, row0, part_len, 0) == request)[:, None]
        key_slots.append(
            jnp.where(
                keep,
                lax.dynamic_slice_in_dim(keys_pad, row0, part_len, 0),
                jnp.zeros((), jnp.bfloat16),
            )
        )
        value_slots.append(
            jnp.where(
                keep,
                lax.dynamic_slice_in_dim(values_pad, row0, part_len, 0),
                jnp.zeros((), jnp.bfloat16),
            )
        )
    return (hidden_out, jnp.stack(key_slots), jnp.stack(value_slots))


def solution(mesh):
    devices = np.asarray(mesh.devices)
    n_seq, n_tensor = devices.shape
    split = Mesh(
        devices.reshape(n_seq // 2, 2, n_tensor // HEADS_PER_DEVICE, HEADS_PER_DEVICE),
        ("sh", "core", "th", "tl"),
    )
    rows = P(("sh", "core", "th", "tl"), None)
    cols = P(None, ("th", "tl"))
    return jax.shard_map(
        on_device,
        mesh=split,
        in_specs=(
            rows,
            P(),
            cols,
            cols,
            cols,
            P(("th", "tl"), None),
            P(),
            P(),
            P(),
            P(),
        ),
        out_specs=(
            rows,
            P(None, ("sh", "core"), ("th", "tl")),
            P(None, ("sh", "core"), ("th", "tl")),
        ),
        check_vma=False,
    )
```

```python
import jax
import jax.numpy as jnp
import numpy as np
from jax import lax
from jax.sharding import Mesh
from jax.sharding import PartitionSpec as P

HD = 128


EPSILON = 1e-06
SOFTCAP = 50.0
QUERY_SCALE = 144.0 ** (-0.5)
SCORE_SHIFT = 20.0
ROPE_BASE = 10000.0
KEY_TILE = 512
Q_CHUNKS = 4
HEADS_PER_DEVICE = 4


def rms_scale(values, gain):
    mean_sq = jnp.mean(values * values, axis=-1, keepdims=True)
    return values * lax.rsqrt(mean_sq + EPSILON) * gain


def rotate(values, positions):
    head_dim = values.shape[-1]
    half_dim = head_dim // 2
    freqs = ROPE_BASE ** (-2.0 * jnp.arange(half_dim, dtype=jnp.float32) / head_dim)
    angles = positions.astype(jnp.float32)[:, None] * freqs[None, :]
    cosine = jnp.cos(angles)[:, None, :]
    sine = jnp.sin(angles)[:, None, :]
    first = values[..., :half_dim]
    second = values[..., half_dim:]
    return jnp.concatenate(
        [first * cosine - second * sine, second * cosine + first * sine], axis=-1
    )


def segment_starts_of(row_segments, seg_lengths):
    starts = jnp.cumsum(seg_lengths) - seg_lengths
    request_ids = jnp.arange(seg_lengths.shape[0], dtype=jnp.int32)
    return jnp.sum(
        jnp.where(row_segments[:, None] == request_ids[None, :], starts[None, :], 0), axis=1
    )


def on_device(
    hidden_in,
    norm_gain,
    query_weight,
    key_weight,
    value_weight,
    out_weight,
    post_gain,
    seg_lengths,
    segment_ids,
    slot_map,
):
    n_group = lax.axis_size("th")
    n_seq = lax.axis_size("seq")
    n_pair = lax.axis_size("tl")
    kv_local = n_pair // 2
    local_rows = hidden_in.shape[0]
    tokens = segment_ids.shape[0]
    group_rows = local_rows * n_group
    seq_rows = group_rows * n_pair
    head_dim = HD
    half_kv = key_weight.shape[1]
    seq_index = lax.axis_index("seq")
    pair_index = lax.axis_index("tl")
    slot_count = seg_lengths.shape[0]

    hidden = hidden_in.astype(jnp.float32)
    normed = rms_scale(hidden, norm_gain).astype(jnp.bfloat16)

    own_joined = jnp.concatenate([query_weight, key_weight, value_weight], axis=1)
    core = seq_index % 2
    fetched = lax.all_gather(
        jnp.where(core == 0, query_weight, jnp.concatenate([key_weight, value_weight], 1)),
        "tl",
        axis=0,
        tiled=False,
    )
    swapped = lax.ppermute(fetched, "seq", [(i, i ^ 1) for i in range(n_seq)])
    pair_out = lax.all_gather(out_weight, "tl", axis=0, tiled=True)

    spread = jnp.broadcast_to(normed[None], (n_group,) + normed.shape)
    gathered = lax.all_to_all(spread, "th", 0, 0, tiled=True).reshape(group_rows, -1)
    width = own_joined.shape[1]
    mixed_fetched = jnp.einsum(
        "rd,cdw->rcw", gathered, fetched, preferred_element_type=jnp.float32
    )
    mixed_swapped = jnp.einsum(
        "rd,cdw->rcw", gathered, swapped, preferred_element_type=jnp.float32
    )
    mixed = jnp.where(
        core == 0,
        jnp.concatenate([mixed_fetched, mixed_swapped], 2),
        jnp.concatenate([mixed_swapped, mixed_fetched], 2),
    )
    queries = mixed[:, :, :head_dim]
    full_key = mixed[:, :, head_dim : head_dim + half_kv].reshape(
        group_rows, kv_local, 2 * half_kv
    )
    full_value = mixed[:, :, head_dim + half_kv :].reshape(group_rows, kv_local, 2 * half_kv)

    member = jnp.arange(group_rows, dtype=jnp.int32) // local_rows
    within = jnp.arange(group_rows, dtype=jnp.int32) % local_rows
    row_ids = seq_index * seq_rows + (member * n_pair + pair_index) * local_rows + within
    row_segments = jnp.take(segment_ids, row_ids)
    positions = row_ids - segment_starts_of(row_segments, seg_lengths)

    q_rot = rotate(queries, positions).astype(jnp.bfloat16)
    k_rot = rotate(full_key, positions).astype(jnp.bfloat16)
    v_bf = full_value.astype(jnp.bfloat16)

    kv = jnp.stack([jnp.transpose(k_rot, (1, 0, 2)), jnp.transpose(v_bf, (1, 0, 2))])
    kv_all = lax.all_gather(kv, ("seq", "tl"), axis=2, tiled=True)
    kv_all = kv_all.reshape(2, kv_local, n_seq, n_pair, n_group, local_rows, head_dim)
    kv_all = jnp.transpose(kv_all, (0, 1, 2, 4, 3, 5, 6)).reshape(2, kv_local, tokens, head_dim)
    key_rows = kv_all[0]
    value_rows = kv_all[1]

    chunk_rows = group_rows // Q_CHUNKS
    member_part = local_rows // Q_CHUNKS
    q_chunks = jnp.transpose(
        q_rot.reshape(n_group, Q_CHUNKS, member_part, n_pair, head_dim), (1, 0, 2, 3, 4)
    ).reshape(Q_CHUNKS, chunk_rows, kv_local, 2, head_dim)
    q_ids = jnp.transpose(row_ids.reshape(n_group, Q_CHUNKS, member_part), (1, 0, 2)).reshape(
        Q_CHUNKS, chunk_rows
    )
    q_segs = jnp.transpose(
        row_segments.reshape(n_group, Q_CHUNKS, member_part), (1, 0, 2)
    ).reshape(Q_CHUNKS, chunk_rows)
    q_pos = jnp.transpose(positions.reshape(n_group, Q_CHUNKS, member_part), (1, 0, 2)).reshape(
        Q_CHUNKS, chunk_rows
    )

    def attend(chunk):
        def tile(tile_index, state):
            numer_one, denom_one = state
            k_start = tile_index * KEY_TILE
            k_block = lax.dynamic_slice_in_dim(key_rows, k_start, KEY_TILE, 1)
            v_block = lax.dynamic_slice_in_dim(value_rows, k_start, KEY_TILE, 1)
            k_segs = lax.dynamic_slice_in_dim(segment_ids, k_start, KEY_TILE, 0)
            k_ids = k_start + jnp.arange(KEY_TILE, dtype=jnp.int32)

            scores = (
                jnp.einsum(
                    "qkgd,ktd->kgqt",
                    q_chunks[chunk],
                    k_block,
                    preferred_element_type=jnp.float32,
                )
                * QUERY_SCALE
            )
            scores = SOFTCAP * jnp.tanh(scores / SOFTCAP)
            live = (k_ids[None, :] <= q_ids[chunk][:, None]) & (
                k_segs[None, :] == q_segs[chunk][:, None]
            )
            weights = jnp.where(live[None, None], jnp.exp(scores - SCORE_SHIFT), 0.0)
            denom_one = denom_one + jnp.sum(weights, axis=-1)
            numer_one = numer_one + jnp.einsum(
                "kgqt,ktd->qkgd",
                weights.astype(jnp.bfloat16),
                v_block,
                preferred_element_type=jnp.float32,
            )
            return (numer_one, denom_one)

        zero_numer = jnp.zeros((chunk_rows, kv_local, 2, head_dim), jnp.float32)
        zero_denom = jnp.zeros((kv_local, 2, chunk_rows), jnp.float32)
        lo_tile = jnp.min(q_ids[chunk] - q_pos[chunk]) // KEY_TILE
        hi_tile = jnp.max(q_ids[chunk]) // KEY_TILE + 1
        numer, denom = lax.fori_loop(lo_tile, hi_tile, tile, (zero_numer, zero_denom))
        denom_rows = jnp.transpose(denom, (2, 0, 1))[..., None]
        attended = (numer / denom_rows).astype(jnp.bfloat16).reshape(
            chunk_rows, n_pair * head_dim
        )
        partial = jnp.dot(attended, pair_out, preferred_element_type=jnp.float32).astype(
            jnp.bfloat16
        )
        pieces = lax.all_to_all(
            partial.reshape(n_group, member_part, -1), "th", 0, 0, tiled=True
        )
        return jnp.sum(pieces.astype(jnp.float32), axis=0)

    projected = jnp.concatenate([attend(chunk) for chunk in range(Q_CHUNKS)], axis=0)
    hidden_out = (hidden + rms_scale(projected, post_gain)).astype(jnp.bfloat16)

    cache_len = tokens // 2
    part_len = cache_len // n_seq
    request_ids = jnp.arange(slot_count, dtype=jnp.int32)
    starts = jnp.cumsum(seg_lengths) - seg_lengths
    own_head = pair_index // 2
    own_offset = pair_index % 2 * half_kv
    own_keys = lax.dynamic_slice_in_dim(
        lax.dynamic_index_in_dim(key_rows, own_head, 0, keepdims=False), own_offset, half_kv, 1
    )
    own_values = lax.dynamic_slice_in_dim(
        lax.dynamic_index_in_dim(value_rows, own_head, 0, keepdims=False), own_offset, half_kv, 1
    )
    keys_pad = jnp.concatenate([own_keys, jnp.zeros((cache_len, half_kv), jnp.bfloat16)], 0)
    values_pad = jnp.concatenate(
        [own_values, jnp.zeros((cache_len, half_kv), jnp.bfloat16)], 0
    )
    seg_pad = jnp.concatenate([segment_ids, jnp.full((cache_len,), -1, jnp.int32)], 0)
    key_slots = []
    value_slots = []
    for slot_index in range(slot_count):
        request = jnp.sum(jnp.where(slot_map == slot_index, request_ids, 0)).astype(jnp.int32)
        first_row = jnp.sum(jnp.where(request_ids == request, starts, 0)).astype(jnp.int32)
        row0 = first_row + seq_index * part_len
        keep = (lax.dynamic_slice_in_dim(seg_pad, row0, part_len, 0) == request)[:, None]
        key_slots.append(
            jnp.where(
                keep,
                lax.dynamic_slice_in_dim(keys_pad, row0, part_len, 0),
                jnp.zeros((), jnp.bfloat16),
            )
        )
        value_slots.append(
            jnp.where(
                keep,
                lax.dynamic_slice_in_dim(values_pad, row0, part_len, 0),
                jnp.zeros((), jnp.bfloat16),
            )
        )
    return (hidden_out, jnp.stack(key_slots), jnp.stack(value_slots))


def solution(mesh):
    devices = np.asarray(mesh.devices)
    n_seq, n_tensor = devices.shape
    split = Mesh(
        devices.reshape(n_seq, n_tensor // HEADS_PER_DEVICE, HEADS_PER_DEVICE),
        ("seq", "th", "tl"),
    )
    rows = P(("seq", "th", "tl"), None)
    cols = P(None, ("th", "tl"))
    return jax.shard_map(
        on_device,
        mesh=split,
        in_specs=(
            rows,
            P(),
            cols,
            cols,
            cols,
            P(("th", "tl"), None),
            P(),
            P(),
            P(),
            P(),
        ),
        out_specs=(rows, P(None, "seq", ("th", "tl")), P(None, "seq", ("th", "tl"))),
        check_vma=False,
    )
```

```python
import jax
import jax.numpy as jnp
import numpy as np
from jax import lax
from jax.sharding import Mesh
from jax.sharding import PartitionSpec as P

HD = 128


EPSILON = 1e-06
SOFTCAP = 50.0
QUERY_SCALE = 144.0 ** (-0.5)
SCORE_SHIFT = 20.0
ROPE_BASE = 10000.0
KEY_TILE = 1024
Q_CHUNKS = 2
HEADS_PER_DEVICE = 4


def rms_scale(values, gain):
    mean_sq = jnp.mean(values * values, axis=-1, keepdims=True)
    return values * lax.rsqrt(mean_sq + EPSILON) * gain


def rotate(values, positions):
    head_dim = values.shape[-1]
    half_dim = head_dim // 2
    freqs = ROPE_BASE ** (-2.0 * jnp.arange(half_dim, dtype=jnp.float32) / head_dim)
    angles = positions.astype(jnp.float32)[:, None] * freqs[None, :]
    cosine = jnp.cos(angles)[:, None, :]
    sine = jnp.sin(angles)[:, None, :]
    first = values[..., :half_dim]
    second = values[..., half_dim:]
    return jnp.concatenate(
        [first * cosine - second * sine, second * cosine + first * sine], axis=-1
    )


def segment_starts_of(row_segments, seg_lengths):
    starts = jnp.cumsum(seg_lengths) - seg_lengths
    request_ids = jnp.arange(seg_lengths.shape[0], dtype=jnp.int32)
    return jnp.sum(
        jnp.where(row_segments[:, None] == request_ids[None, :], starts[None, :], 0), axis=1
    )


def on_device(
    hidden_in,
    norm_gain,
    query_weight,
    key_weight,
    value_weight,
    out_weight,
    post_gain,
    seg_lengths,
    segment_ids,
    slot_map,
):
    n_group = lax.axis_size("th")
    n_seq = lax.axis_size("seq")
    n_pair = lax.axis_size("tl")
    kv_local = n_pair // 2
    local_rows = hidden_in.shape[0]
    tokens = segment_ids.shape[0]
    group_rows = local_rows * n_group
    seq_rows = group_rows * n_pair
    head_dim = HD
    half_kv = key_weight.shape[1]
    seq_index = lax.axis_index("seq")
    pair_index = lax.axis_index("tl")
    slot_count = seg_lengths.shape[0]

    hidden = hidden_in.astype(jnp.float32)
    normed = rms_scale(hidden, norm_gain).astype(jnp.bfloat16)

    own_joined = jnp.concatenate([query_weight, key_weight, value_weight], axis=1)
    core = seq_index % 2
    fetched = lax.all_gather(
        jnp.where(core == 0, query_weight, jnp.concatenate([key_weight, value_weight], 1)),
        "tl",
        axis=0,
        tiled=False,
    )
    swapped = lax.ppermute(fetched, "seq", [(i, i ^ 1) for i in range(n_seq)])
    pair_out = lax.all_gather(out_weight, "tl", axis=0, tiled=True)

    spread = jnp.broadcast_to(normed[None], (n_group,) + normed.shape)
    gathered = lax.all_to_all(spread, "th", 0, 0, tiled=True).reshape(group_rows, -1)
    width = own_joined.shape[1]
    mixed_fetched = jnp.einsum(
        "rd,cdw->rcw", gathered, fetched, preferred_element_type=jnp.float32
    )
    mixed_swapped = jnp.einsum(
        "rd,cdw->rcw", gathered, swapped, preferred_element_type=jnp.float32
    )
    mixed = jnp.where(
        core == 0,
        jnp.concatenate([mixed_fetched, mixed_swapped], 2),
        jnp.concatenate([mixed_swapped, mixed_fetched], 2),
    )
    queries = mixed[:, :, :head_dim]
    full_key = mixed[:, :, head_dim : head_dim + half_kv].reshape(
        group_rows, kv_local, 2 * half_kv
    )
    full_value = mixed[:, :, head_dim + half_kv :].reshape(group_rows, kv_local, 2 * half_kv)

    member = jnp.arange(group_rows, dtype=jnp.int32) // local_rows
    within = jnp.arange(group_rows, dtype=jnp.int32) % local_rows
    row_ids = seq_index * seq_rows + (member * n_pair + pair_index) * local_rows + within
    row_segments = jnp.take(segment_ids, row_ids)
    positions = row_ids - segment_starts_of(row_segments, seg_lengths)

    q_rot = rotate(queries, positions).astype(jnp.bfloat16)
    k_rot = rotate(full_key, positions).astype(jnp.bfloat16)
    v_bf = full_value.astype(jnp.bfloat16)

    kv = jnp.stack([jnp.transpose(k_rot, (1, 0, 2)), jnp.transpose(v_bf, (1, 0, 2))])
    kv_all = lax.all_gather(kv, ("seq", "tl"), axis=2, tiled=True)
    kv_all = kv_all.reshape(2, kv_local, n_seq, n_pair, n_group, local_rows, head_dim)
    kv_all = jnp.transpose(kv_all, (0, 1, 2, 4, 3, 5, 6)).reshape(2, kv_local, tokens, head_dim)
    key_rows = kv_all[0]
    value_rows = kv_all[1]

    chunk_rows = group_rows // Q_CHUNKS
    member_part = local_rows // Q_CHUNKS
    q_chunks = jnp.transpose(
        q_rot.reshape(n_group, Q_CHUNKS, member_part, n_pair, head_dim), (1, 0, 2, 3, 4)
    ).reshape(Q_CHUNKS, chunk_rows, kv_local, 2, head_dim)
    q_ids = jnp.transpose(row_ids.reshape(n_group, Q_CHUNKS, member_part), (1, 0, 2)).reshape(
        Q_CHUNKS, chunk_rows
    )
    q_segs = jnp.transpose(
        row_segments.reshape(n_group, Q_CHUNKS, member_part), (1, 0, 2)
    ).reshape(Q_CHUNKS, chunk_rows)
    q_pos = jnp.transpose(positions.reshape(n_group, Q_CHUNKS, member_part), (1, 0, 2)).reshape(
        Q_CHUNKS, chunk_rows
    )

    def attend(chunk):
        def tile(tile_index, state):
            numer_one, denom_one = state
            k_start = tile_index * KEY_TILE
            k_block = lax.dynamic_slice_in_dim(key_rows, k_start, KEY_TILE, 1)
            v_block = lax.dynamic_slice_in_dim(value_rows, k_start, KEY_TILE, 1)
            k_segs = lax.dynamic_slice_in_dim(segment_ids, k_start, KEY_TILE, 0)
            k_ids = k_start + jnp.arange(KEY_TILE, dtype=jnp.int32)

            scores = (
                jnp.einsum(
                    "qkgd,ktd->kgqt",
                    q_chunks[chunk],
                    k_block,
                    preferred_element_type=jnp.float32,
                )
                * QUERY_SCALE
            )
            scores = SOFTCAP * jnp.tanh(scores / SOFTCAP)
            live = (k_ids[None, :] <= q_ids[chunk][:, None]) & (
                k_segs[None, :] == q_segs[chunk][:, None]
            )
            weights = jnp.where(live[None, None], jnp.exp(scores - SCORE_SHIFT), 0.0)
            denom_one = denom_one + jnp.sum(weights, axis=-1)
            numer_one = numer_one + jnp.einsum(
                "kgqt,ktd->qkgd",
                weights.astype(jnp.bfloat16),
                v_block,
                preferred_element_type=jnp.float32,
            )
            return (numer_one, denom_one)

        zero_numer = jnp.zeros((chunk_rows, kv_local, 2, head_dim), jnp.float32)
        zero_denom = jnp.zeros((kv_local, 2, chunk_rows), jnp.float32)
        lo_tile = jnp.min(q_ids[chunk] - q_pos[chunk]) // KEY_TILE
        hi_tile = jnp.max(q_ids[chunk]) // KEY_TILE + 1
        numer, denom = lax.fori_loop(lo_tile, hi_tile, tile, (zero_numer, zero_denom))
        denom_rows = jnp.transpose(denom, (2, 0, 1))[..., None]
        attended = (numer / denom_rows).astype(jnp.bfloat16).reshape(
            chunk_rows, n_pair * head_dim
        )
        partial = jnp.dot(attended, pair_out, preferred_element_type=jnp.float32).astype(
            jnp.bfloat16
        )
        pieces = lax.all_to_all(
            partial.reshape(n_group, member_part, -1), "th", 0, 0, tiled=True
        )
        return jnp.sum(pieces.astype(jnp.float32), axis=0)

    projected = jnp.concatenate([attend(chunk) for chunk in range(Q_CHUNKS)], axis=0)
    hidden_out = (hidden + rms_scale(projected, post_gain)).astype(jnp.bfloat16)

    cache_len = tokens // 2
    part_len = cache_len // n_seq
    request_ids = jnp.arange(slot_count, dtype=jnp.int32)
    starts = jnp.cumsum(seg_lengths) - seg_lengths
    own_head = pair_index // 2
    own_offset = pair_index % 2 * half_kv
    own_keys = lax.dynamic_slice_in_dim(
        lax.dynamic_index_in_dim(key_rows, own_head, 0, keepdims=False), own_offset, half_kv, 1
    )
    own_values = lax.dynamic_slice_in_dim(
        lax.dynamic_index_in_dim(value_rows, own_head, 0, keepdims=False), own_offset, half_kv, 1
    )
    keys_pad = jnp.concatenate([own_keys, jnp.zeros((cache_len, half_kv), jnp.bfloat16)], 0)
    values_pad = jnp.concatenate(
        [own_values, jnp.zeros((cache_len, half_kv), jnp.bfloat16)], 0
    )
    seg_pad = jnp.concatenate([segment_ids, jnp.full((cache_len,), -1, jnp.int32)], 0)
    key_slots = []
    value_slots = []
    for slot_index in range(slot_count):
        request = jnp.sum(jnp.where(slot_map == slot_index, request_ids, 0)).astype(jnp.int32)
        first_row = jnp.sum(jnp.where(request_ids == request, starts, 0)).astype(jnp.int32)
        row0 = first_row + seq_index * part_len
        keep = (lax.dynamic_slice_in_dim(seg_pad, row0, part_len, 0) == request)[:, None]
        key_slots.append(
            jnp.where(
                keep,
                lax.dynamic_slice_in_dim(keys_pad, row0, part_len, 0),
                jnp.zeros((), jnp.bfloat16),
            )
        )
        value_slots.append(
            jnp.where(
                keep,
                lax.dynamic_slice_in_dim(values_pad, row0, part_len, 0),
                jnp.zeros((), jnp.bfloat16),
            )
        )
    return (hidden_out, jnp.stack(key_slots), jnp.stack(value_slots))


def solution(mesh):
    devices = np.asarray(mesh.devices)
    n_seq, n_tensor = devices.shape
    split = Mesh(
        devices.reshape(n_seq, n_tensor // HEADS_PER_DEVICE, HEADS_PER_DEVICE),
        ("seq", "th", "tl"),
    )
    rows = P(("seq", "th", "tl"), None)
    cols = P(None, ("th", "tl"))
    return jax.shard_map(
        on_device,
        mesh=split,
        in_specs=(
            rows,
            P(),
            cols,
            cols,
            cols,
            P(("th", "tl"), None),
            P(),
            P(),
            P(),
            P(),
        ),
        out_specs=(rows, P(None, "seq", ("th", "tl")), P(None, "seq", ("th", "tl"))),
        check_vma=False,
    )
```

```python
import jax
import jax.numpy as jnp
import numpy as np
from jax import lax
from jax.sharding import Mesh
from jax.sharding import PartitionSpec as P

HD = 128


EPSILON = 1e-06
SOFTCAP = 50.0
QUERY_SCALE = 144.0 ** (-0.5)
SCORE_SHIFT = 20.0
ROPE_BASE = 10000.0
KEY_TILE = 2048
Q_CHUNKS = 2
HEADS_PER_DEVICE = 4


def rms_scale(values, gain):
    mean_sq = jnp.mean(values * values, axis=-1, keepdims=True)
    return values * lax.rsqrt(mean_sq + EPSILON) * gain


def rotate(values, positions):
    head_dim = values.shape[-1]
    half_dim = head_dim // 2
    freqs = ROPE_BASE ** (-2.0 * jnp.arange(half_dim, dtype=jnp.float32) / head_dim)
    angles = positions.astype(jnp.float32)[:, None] * freqs[None, :]
    cosine = jnp.cos(angles)[:, None, :]
    sine = jnp.sin(angles)[:, None, :]
    first = values[..., :half_dim]
    second = values[..., half_dim:]
    return jnp.concatenate(
        [first * cosine - second * sine, second * cosine + first * sine], axis=-1
    )


def segment_starts_of(row_segments, seg_lengths):
    starts = jnp.cumsum(seg_lengths) - seg_lengths
    request_ids = jnp.arange(seg_lengths.shape[0], dtype=jnp.int32)
    return jnp.sum(
        jnp.where(row_segments[:, None] == request_ids[None, :], starts[None, :], 0), axis=1
    )


def on_device(
    hidden_in,
    norm_gain,
    query_weight,
    key_weight,
    value_weight,
    out_weight,
    post_gain,
    seg_lengths,
    segment_ids,
    slot_map,
):
    n_group = lax.axis_size("th")
    n_seq = lax.axis_size("seq")
    n_pair = lax.axis_size("tl")
    kv_local = n_pair // 2
    local_rows = hidden_in.shape[0]
    tokens = segment_ids.shape[0]
    group_rows = local_rows * n_group
    seq_rows = group_rows * n_pair
    head_dim = HD
    half_kv = key_weight.shape[1]
    seq_index = lax.axis_index("seq")
    pair_index = lax.axis_index("tl")
    slot_count = seg_lengths.shape[0]

    hidden = hidden_in.astype(jnp.float32)
    normed = rms_scale(hidden, norm_gain).astype(jnp.bfloat16)

    own_joined = jnp.concatenate([query_weight, key_weight, value_weight], axis=1)
    core = seq_index % 2
    fetched = lax.all_gather(
        jnp.where(core == 0, query_weight, jnp.concatenate([key_weight, value_weight], 1)),
        "tl",
        axis=0,
        tiled=False,
    )
    swapped = lax.ppermute(fetched, "seq", [(i, i ^ 1) for i in range(n_seq)])
    pair_out = lax.all_gather(out_weight, "tl", axis=0, tiled=True)

    spread = jnp.broadcast_to(normed[None], (n_group,) + normed.shape)
    gathered = lax.all_to_all(spread, "th", 0, 0, tiled=True).reshape(group_rows, -1)
    width = own_joined.shape[1]
    mixed_fetched = jnp.einsum(
        "rd,cdw->rcw", gathered, fetched, preferred_element_type=jnp.float32
    )
    mixed_swapped = jnp.einsum(
        "rd,cdw->rcw", gathered, swapped, preferred_element_type=jnp.float32
    )
    mixed = jnp.where(
        core == 0,
        jnp.concatenate([mixed_fetched, mixed_swapped], 2),
        jnp.concatenate([mixed_swapped, mixed_fetched], 2),
    )
    queries = mixed[:, :, :head_dim]
    full_key = mixed[:, :, head_dim : head_dim + half_kv].reshape(
        group_rows, kv_local, 2 * half_kv
    )
    full_value = mixed[:, :, head_dim + half_kv :].reshape(group_rows, kv_local, 2 * half_kv)

    member = jnp.arange(group_rows, dtype=jnp.int32) // local_rows
    within = jnp.arange(group_rows, dtype=jnp.int32) % local_rows
    row_ids = seq_index * seq_rows + (member * n_pair + pair_index) * local_rows + within
    row_segments = jnp.take(segment_ids, row_ids)
    positions = row_ids - segment_starts_of(row_segments, seg_lengths)

    q_rot = rotate(queries, positions).astype(jnp.bfloat16)
    k_rot = rotate(full_key, positions).astype(jnp.bfloat16)
    v_bf = full_value.astype(jnp.bfloat16)

    kv = jnp.stack([jnp.transpose(k_rot, (1, 0, 2)), jnp.transpose(v_bf, (1, 0, 2))])
    kv_all = lax.all_gather(kv, ("seq", "tl"), axis=2, tiled=True)
    kv_all = kv_all.reshape(2, kv_local, n_seq, n_pair, n_group, local_rows, head_dim)
    kv_all = jnp.transpose(kv_all, (0, 1, 2, 4, 3, 5, 6)).reshape(2, kv_local, tokens, head_dim)
    key_rows = kv_all[0]
    value_rows = kv_all[1]

    chunk_rows = group_rows // Q_CHUNKS
    member_part = local_rows // Q_CHUNKS
    q_chunks = jnp.transpose(
        q_rot.reshape(n_group, Q_CHUNKS, member_part, n_pair, head_dim), (1, 0, 2, 3, 4)
    ).reshape(Q_CHUNKS, chunk_rows, kv_local, 2, head_dim)
    q_ids = jnp.transpose(row_ids.reshape(n_group, Q_CHUNKS, member_part), (1, 0, 2)).reshape(
        Q_CHUNKS, chunk_rows
    )
    q_segs = jnp.transpose(
        row_segments.reshape(n_group, Q_CHUNKS, member_part), (1, 0, 2)
    ).reshape(Q_CHUNKS, chunk_rows)
    q_pos = jnp.transpose(positions.reshape(n_group, Q_CHUNKS, member_part), (1, 0, 2)).reshape(
        Q_CHUNKS, chunk_rows
    )

    def attend(chunk):
        def tile(tile_index, state):
            numer_one, denom_one = state
            k_start = tile_index * KEY_TILE
            k_block = lax.dynamic_slice_in_dim(key_rows, k_start, KEY_TILE, 1)
            v_block = lax.dynamic_slice_in_dim(value_rows, k_start, KEY_TILE, 1)
            k_segs = lax.dynamic_slice_in_dim(segment_ids, k_start, KEY_TILE, 0)
            k_ids = k_start + jnp.arange(KEY_TILE, dtype=jnp.int32)

            scores = (
                jnp.einsum(
                    "qkgd,ktd->kgqt",
                    q_chunks[chunk],
                    k_block,
                    preferred_element_type=jnp.float32,
                )
                * QUERY_SCALE
            )
            scores = SOFTCAP * jnp.tanh(scores / SOFTCAP)
            live = (k_ids[None, :] <= q_ids[chunk][:, None]) & (
                k_segs[None, :] == q_segs[chunk][:, None]
            )
            weights = jnp.where(live[None, None], jnp.exp(scores - SCORE_SHIFT), 0.0)
            denom_one = denom_one + jnp.sum(weights, axis=-1)
            numer_one = numer_one + jnp.einsum(
                "kgqt,ktd->qkgd",
                weights.astype(jnp.bfloat16),
                v_block,
                preferred_element_type=jnp.float32,
            )
            return (numer_one, denom_one)

        zero_numer = jnp.zeros((chunk_rows, kv_local, 2, head_dim), jnp.float32)
        zero_denom = jnp.zeros((kv_local, 2, chunk_rows), jnp.float32)
        lo_tile = jnp.min(q_ids[chunk] - q_pos[chunk]) // KEY_TILE
        hi_tile = jnp.max(q_ids[chunk]) // KEY_TILE + 1
        numer, denom = lax.fori_loop(lo_tile, hi_tile, tile, (zero_numer, zero_denom))
        denom_rows = jnp.transpose(denom, (2, 0, 1))[..., None]
        attended = (numer / denom_rows).astype(jnp.bfloat16).reshape(
            chunk_rows, n_pair * head_dim
        )
        partial = jnp.dot(attended, pair_out, preferred_element_type=jnp.float32).astype(
            jnp.bfloat16
        )
        pieces = lax.all_to_all(
            partial.reshape(n_group, member_part, -1), "th", 0, 0, tiled=True
        )
        return jnp.sum(pieces.astype(jnp.float32), axis=0)

    projected = jnp.concatenate([attend(chunk) for chunk in range(Q_CHUNKS)], axis=0)
    hidden_out = (hidden + rms_scale(projected, post_gain)).astype(jnp.bfloat16)

    cache_len = tokens // 2
    part_len = cache_len // n_seq
    request_ids = jnp.arange(slot_count, dtype=jnp.int32)
    starts = jnp.cumsum(seg_lengths) - seg_lengths
    own_head = pair_index // 2
    own_offset = pair_index % 2 * half_kv
    own_keys = lax.dynamic_slice_in_dim(
        lax.dynamic_index_in_dim(key_rows, own_head, 0, keepdims=False), own_offset, half_kv, 1
    )
    own_values = lax.dynamic_slice_in_dim(
        lax.dynamic_index_in_dim(value_rows, own_head, 0, keepdims=False), own_offset, half_kv, 1
    )
    keys_pad = jnp.concatenate([own_keys, jnp.zeros((cache_len, half_kv), jnp.bfloat16)], 0)
    values_pad = jnp.concatenate(
        [own_values, jnp.zeros((cache_len, half_kv), jnp.bfloat16)], 0
    )
    seg_pad = jnp.concatenate([segment_ids, jnp.full((cache_len,), -1, jnp.int32)], 0)
    key_slots = []
    value_slots = []
    for slot_index in range(slot_count):
        request = jnp.sum(jnp.where(slot_map == slot_index, request_ids, 0)).astype(jnp.int32)
        first_row = jnp.sum(jnp.where(request_ids == request, starts, 0)).astype(jnp.int32)
        row0 = first_row + seq_index * part_len
        keep = (lax.dynamic_slice_in_dim(seg_pad, row0, part_len, 0) == request)[:, None]
        key_slots.append(
            jnp.where(
                keep,
                lax.dynamic_slice_in_dim(keys_pad, row0, part_len, 0),
                jnp.zeros((), jnp.bfloat16),
            )
        )
        value_slots.append(
            jnp.where(
                keep,
                lax.dynamic_slice_in_dim(values_pad, row0, part_len, 0),
                jnp.zeros((), jnp.bfloat16),
            )
        )
    return (hidden_out, jnp.stack(key_slots), jnp.stack(value_slots))


def solution(mesh):
    devices = np.asarray(mesh.devices)
    n_seq, n_tensor = devices.shape
    split = Mesh(
        devices.reshape(n_seq, n_tensor // HEADS_PER_DEVICE, HEADS_PER_DEVICE),
        ("seq", "th", "tl"),
    )
    rows = P(("seq", "th", "tl"), None)
    cols = P(None, ("th", "tl"))
    return jax.shard_map(
        on_device,
        mesh=split,
        in_specs=(
            rows,
            P(),
            cols,
            cols,
            cols,
            P(("th", "tl"), None),
            P(),
            P(),
            P(),
            P(),
        ),
        out_specs=(rows, P(None, "seq", ("th", "tl")), P(None, "seq", ("th", "tl"))),
        check_vma=False,
    )
```

```python
import jax
import jax.numpy as jnp
import numpy as np
from jax import lax
from jax.sharding import Mesh
from jax.sharding import PartitionSpec as P

HD = 128


EPSILON = 1e-06
SOFTCAP = 50.0
QUERY_SCALE = 144.0 ** (-0.5)
SCORE_SHIFT = 20.0
ROPE_BASE = 10000.0
KEY_TILE = 1024
Q_CHUNKS = 1
HEADS_PER_DEVICE = 4


def rms_scale(values, gain):
    mean_sq = jnp.mean(values * values, axis=-1, keepdims=True)
    return values * lax.rsqrt(mean_sq + EPSILON) * gain


def rotate(values, positions):
    head_dim = values.shape[-1]
    half_dim = head_dim // 2
    freqs = ROPE_BASE ** (-2.0 * jnp.arange(half_dim, dtype=jnp.float32) / head_dim)
    angles = positions.astype(jnp.float32)[:, None] * freqs[None, :]
    cosine = jnp.cos(angles)[:, None, :]
    sine = jnp.sin(angles)[:, None, :]
    first = values[..., :half_dim]
    second = values[..., half_dim:]
    return jnp.concatenate(
        [first * cosine - second * sine, second * cosine + first * sine], axis=-1
    )


def segment_starts_of(row_segments, seg_lengths):
    starts = jnp.cumsum(seg_lengths) - seg_lengths
    request_ids = jnp.arange(seg_lengths.shape[0], dtype=jnp.int32)
    return jnp.sum(
        jnp.where(row_segments[:, None] == request_ids[None, :], starts[None, :], 0), axis=1
    )


def on_device(
    hidden_in,
    norm_gain,
    query_weight,
    key_weight,
    value_weight,
    out_weight,
    post_gain,
    seg_lengths,
    segment_ids,
    slot_map,
):
    n_group = lax.axis_size("th")
    n_seq = lax.axis_size("seq")
    n_pair = lax.axis_size("tl")
    kv_local = n_pair // 2
    local_rows = hidden_in.shape[0]
    tokens = segment_ids.shape[0]
    group_rows = local_rows * n_group
    seq_rows = group_rows * n_pair
    head_dim = HD
    half_kv = key_weight.shape[1]
    seq_index = lax.axis_index("seq")
    pair_index = lax.axis_index("tl")
    slot_count = seg_lengths.shape[0]

    hidden = hidden_in.astype(jnp.float32)
    normed = rms_scale(hidden, norm_gain).astype(jnp.bfloat16)

    own_joined = jnp.concatenate([query_weight, key_weight, value_weight], axis=1)
    core = seq_index % 2
    fetched = lax.all_gather(
        jnp.where(core == 0, query_weight, jnp.concatenate([key_weight, value_weight], 1)),
        "tl",
        axis=0,
        tiled=False,
    )
    swapped = lax.ppermute(fetched, "seq", [(i, i ^ 1) for i in range(n_seq)])
    pair_out = lax.all_gather(out_weight, "tl", axis=0, tiled=True)

    spread = jnp.broadcast_to(normed[None], (n_group,) + normed.shape)
    gathered = lax.all_to_all(spread, "th", 0, 0, tiled=True).reshape(group_rows, -1)
    width = own_joined.shape[1]
    mixed_fetched = jnp.einsum(
        "rd,cdw->rcw", gathered, fetched, preferred_element_type=jnp.float32
    )
    mixed_swapped = jnp.einsum(
        "rd,cdw->rcw", gathered, swapped, preferred_element_type=jnp.float32
    )
    mixed = jnp.where(
        core == 0,
        jnp.concatenate([mixed_fetched, mixed_swapped], 2),
        jnp.concatenate([mixed_swapped, mixed_fetched], 2),
    )
    queries = mixed[:, :, :head_dim]
    full_key = mixed[:, :, head_dim : head_dim + half_kv].reshape(
        group_rows, kv_local, 2 * half_kv
    )
    full_value = mixed[:, :, head_dim + half_kv :].reshape(group_rows, kv_local, 2 * half_kv)

    member = jnp.arange(group_rows, dtype=jnp.int32) // local_rows
    within = jnp.arange(group_rows, dtype=jnp.int32) % local_rows
    row_ids = seq_index * seq_rows + (member * n_pair + pair_index) * local_rows + within
    row_segments = jnp.take(segment_ids, row_ids)
    positions = row_ids - segment_starts_of(row_segments, seg_lengths)

    q_rot = rotate(queries, positions).astype(jnp.bfloat16)
    k_rot = rotate(full_key, positions).astype(jnp.bfloat16)
    v_bf = full_value.astype(jnp.bfloat16)

    kv = jnp.stack([jnp.transpose(k_rot, (1, 0, 2)), jnp.transpose(v_bf, (1, 0, 2))])
    kv_all = lax.all_gather(kv, ("seq", "tl"), axis=2, tiled=True)
    kv_all = kv_all.reshape(2, kv_local, n_seq, n_pair, n_group, local_rows, head_dim)
    kv_all = jnp.transpose(kv_all, (0, 1, 2, 4, 3, 5, 6)).reshape(2, kv_local, tokens, head_dim)
    key_rows = kv_all[0]
    value_rows = kv_all[1]

    chunk_rows = group_rows // Q_CHUNKS
    member_part = local_rows // Q_CHUNKS
    q_chunks = jnp.transpose(
        q_rot.reshape(n_group, Q_CHUNKS, member_part, n_pair, head_dim), (1, 0, 2, 3, 4)
    ).reshape(Q_CHUNKS, chunk_rows, kv_local, 2, head_dim)
    q_ids = jnp.transpose(row_ids.reshape(n_group, Q_CHUNKS, member_part), (1, 0, 2)).reshape(
        Q_CHUNKS, chunk_rows
    )
    q_segs = jnp.transpose(
        row_segments.reshape(n_group, Q_CHUNKS, member_part), (1, 0, 2)
    ).reshape(Q_CHUNKS, chunk_rows)
    q_pos = jnp.transpose(positions.reshape(n_group, Q_CHUNKS, member_part), (1, 0, 2)).reshape(
        Q_CHUNKS, chunk_rows
    )

    def attend(chunk):
        def tile(tile_index, state):
            numer_one, denom_one = state
            k_start = tile_index * KEY_TILE
            k_block = lax.dynamic_slice_in_dim(key_rows, k_start, KEY_TILE, 1)
            v_block = lax.dynamic_slice_in_dim(value_rows, k_start, KEY_TILE, 1)
            k_segs = lax.dynamic_slice_in_dim(segment_ids, k_start, KEY_TILE, 0)
            k_ids = k_start + jnp.arange(KEY_TILE, dtype=jnp.int32)

            scores = (
                jnp.einsum(
                    "qkgd,ktd->kgqt",
                    q_chunks[chunk],
                    k_block,
                    preferred_element_type=jnp.float32,
                )
                * QUERY_SCALE
            )
            scores = SOFTCAP * jnp.tanh(scores / SOFTCAP)
            live = (k_ids[None, :] <= q_ids[chunk][:, None]) & (
                k_segs[None, :] == q_segs[chunk][:, None]
            )
            weights = jnp.where(live[None, None], jnp.exp(scores - SCORE_SHIFT), 0.0)
            denom_one = denom_one + jnp.sum(weights, axis=-1)
            numer_one = numer_one + jnp.einsum(
                "kgqt,ktd->qkgd",
                weights.astype(jnp.bfloat16),
                v_block,
                preferred_element_type=jnp.float32,
            )
            return (numer_one, denom_one)

        zero_numer = jnp.zeros((chunk_rows, kv_local, 2, head_dim), jnp.float32)
        zero_denom = jnp.zeros((kv_local, 2, chunk_rows), jnp.float32)
        lo_tile = jnp.min(q_ids[chunk] - q_pos[chunk]) // KEY_TILE
        hi_tile = jnp.max(q_ids[chunk]) // KEY_TILE + 1
        numer, denom = lax.fori_loop(lo_tile, hi_tile, tile, (zero_numer, zero_denom))
        denom_rows = jnp.transpose(denom, (2, 0, 1))[..., None]
        attended = (numer / denom_rows).astype(jnp.bfloat16).reshape(
            chunk_rows, n_pair * head_dim
        )
        partial = jnp.dot(attended, pair_out, preferred_element_type=jnp.float32).astype(
            jnp.bfloat16
        )
        pieces = lax.all_to_all(
            partial.reshape(n_group, member_part, -1), "th", 0, 0, tiled=True
        )
        return jnp.sum(pieces.astype(jnp.float32), axis=0)

    projected = jnp.concatenate([attend(chunk) for chunk in range(Q_CHUNKS)], axis=0)
    hidden_out = (hidden + rms_scale(projected, post_gain)).astype(jnp.bfloat16)

    cache_len = tokens // 2
    part_len = cache_len // n_seq
    request_ids = jnp.arange(slot_count, dtype=jnp.int32)
    starts = jnp.cumsum(seg_lengths) - seg_lengths
    own_head = pair_index // 2
    own_offset = pair_index % 2 * half_kv
    own_keys = lax.dynamic_slice_in_dim(
        lax.dynamic_index_in_dim(key_rows, own_head, 0, keepdims=False), own_offset, half_kv, 1
    )
    own_values = lax.dynamic_slice_in_dim(
        lax.dynamic_index_in_dim(value_rows, own_head, 0, keepdims=False), own_offset, half_kv, 1
    )
    keys_pad = jnp.concatenate([own_keys, jnp.zeros((cache_len, half_kv), jnp.bfloat16)], 0)
    values_pad = jnp.concatenate(
        [own_values, jnp.zeros((cache_len, half_kv), jnp.bfloat16)], 0
    )
    seg_pad = jnp.concatenate([segment_ids, jnp.full((cache_len,), -1, jnp.int32)], 0)
    key_slots = []
    value_slots = []
    for slot_index in range(slot_count):
        request = jnp.sum(jnp.where(slot_map == slot_index, request_ids, 0)).astype(jnp.int32)
        first_row = jnp.sum(jnp.where(request_ids == request, starts, 0)).astype(jnp.int32)
        row0 = first_row + seq_index * part_len
        keep = (lax.dynamic_slice_in_dim(seg_pad, row0, part_len, 0) == request)[:, None]
        key_slots.append(
            jnp.where(
                keep,
                lax.dynamic_slice_in_dim(keys_pad, row0, part_len, 0),
                jnp.zeros((), jnp.bfloat16),
            )
        )
        value_slots.append(
            jnp.where(
                keep,
                lax.dynamic_slice_in_dim(values_pad, row0, part_len, 0),
                jnp.zeros((), jnp.bfloat16),
            )
        )
    return (hidden_out, jnp.stack(key_slots), jnp.stack(value_slots))


def solution(mesh):
    devices = np.asarray(mesh.devices)
    n_seq, n_tensor = devices.shape
    split = Mesh(
        devices.reshape(n_seq, n_tensor // HEADS_PER_DEVICE, HEADS_PER_DEVICE),
        ("seq", "th", "tl"),
    )
    rows = P(("seq", "th", "tl"), None)
    cols = P(None, ("th", "tl"))
    return jax.shard_map(
        on_device,
        mesh=split,
        in_specs=(
            rows,
            P(),
            cols,
            cols,
            cols,
            P(("th", "tl"), None),
            P(),
            P(),
            P(),
            P(),
        ),
        out_specs=(rows, P(None, "seq", ("th", "tl")), P(None, "seq", ("th", "tl"))),
        check_vma=False,
    )
```

```python
import jax
import jax.numpy as jnp
import numpy as np
from jax import lax
from jax.sharding import Mesh
from jax.sharding import PartitionSpec as P

HD = 128


EPSILON = 1e-06
SOFTCAP = 50.0
QUERY_SCALE = 144.0 ** (-0.5)
SCORE_SHIFT = 20.0
ROPE_BASE = 10000.0
KEY_TILE = 2048
Q_CHUNKS = 1
HEADS_PER_DEVICE = 4


def rms_scale(values, gain):
    mean_sq = jnp.mean(values * values, axis=-1, keepdims=True)
    return values * lax.rsqrt(mean_sq + EPSILON) * gain


def rotate(values, positions):
    head_dim = values.shape[-1]
    half_dim = head_dim // 2
    freqs = ROPE_BASE ** (-2.0 * jnp.arange(half_dim, dtype=jnp.float32) / head_dim)
    angles = positions.astype(jnp.float32)[:, None] * freqs[None, :]
    cosine = jnp.cos(angles)[:, None, :]
    sine = jnp.sin(angles)[:, None, :]
    first = values[..., :half_dim]
    second = values[..., half_dim:]
    return jnp.concatenate(
        [first * cosine - second * sine, second * cosine + first * sine], axis=-1
    )


def segment_starts_of(row_segments, seg_lengths):
    starts = jnp.cumsum(seg_lengths) - seg_lengths
    request_ids = jnp.arange(seg_lengths.shape[0], dtype=jnp.int32)
    return jnp.sum(
        jnp.where(row_segments[:, None] == request_ids[None, :], starts[None, :], 0), axis=1
    )


def on_device(
    hidden_in,
    norm_gain,
    query_weight,
    key_weight,
    value_weight,
    out_weight,
    post_gain,
    seg_lengths,
    segment_ids,
    slot_map,
):
    n_group = lax.axis_size("th")
    n_seq = lax.axis_size("seq")
    n_pair = lax.axis_size("tl")
    kv_local = n_pair // 2
    local_rows = hidden_in.shape[0]
    tokens = segment_ids.shape[0]
    group_rows = local_rows * n_group
    seq_rows = group_rows * n_pair
    head_dim = HD
    half_kv = key_weight.shape[1]
    seq_index = lax.axis_index("seq")
    pair_index = lax.axis_index("tl")
    slot_count = seg_lengths.shape[0]

    hidden = hidden_in.astype(jnp.float32)
    normed = rms_scale(hidden, norm_gain).astype(jnp.bfloat16)

    own_joined = jnp.concatenate([query_weight, key_weight, value_weight], axis=1)
    core = seq_index % 2
    fetched = lax.all_gather(
        jnp.where(core == 0, query_weight, jnp.concatenate([key_weight, value_weight], 1)),
        "tl",
        axis=0,
        tiled=False,
    )
    swapped = lax.ppermute(fetched, "seq", [(i, i ^ 1) for i in range(n_seq)])
    pair_out = lax.all_gather(out_weight, "tl", axis=0, tiled=True)

    spread = jnp.broadcast_to(normed[None], (n_group,) + normed.shape)
    gathered = lax.all_to_all(spread, "th", 0, 0, tiled=True).reshape(group_rows, -1)
    width = own_joined.shape[1]
    mixed_fetched = jnp.einsum(
        "rd,cdw->rcw", gathered, fetched, preferred_element_type=jnp.float32
    )
    mixed_swapped = jnp.einsum(
        "rd,cdw->rcw", gathered, swapped, preferred_element_type=jnp.float32
    )
    mixed = jnp.where(
        core == 0,
        jnp.concatenate([mixed_fetched, mixed_swapped], 2),
        jnp.concatenate([mixed_swapped, mixed_fetched], 2),
    )
    queries = mixed[:, :, :head_dim]
    full_key = mixed[:, :, head_dim : head_dim + half_kv].reshape(
        group_rows, kv_local, 2 * half_kv
    )
    full_value = mixed[:, :, head_dim + half_kv :].reshape(group_rows, kv_local, 2 * half_kv)

    member = jnp.arange(group_rows, dtype=jnp.int32) // local_rows
    within = jnp.arange(group_rows, dtype=jnp.int32) % local_rows
    row_ids = seq_index * seq_rows + (member * n_pair + pair_index) * local_rows + within
    row_segments = jnp.take(segment_ids, row_ids)
    positions = row_ids - segment_starts_of(row_segments, seg_lengths)

    q_rot = rotate(queries, positions).astype(jnp.bfloat16)
    k_rot = rotate(full_key, positions).astype(jnp.bfloat16)
    v_bf = full_value.astype(jnp.bfloat16)

    kv = jnp.stack([jnp.transpose(k_rot, (1, 0, 2)), jnp.transpose(v_bf, (1, 0, 2))])
    kv_all = lax.all_gather(kv, ("seq", "tl"), axis=2, tiled=True)
    kv_all = kv_all.reshape(2, kv_local, n_seq, n_pair, n_group, local_rows, head_dim)
    kv_all = jnp.transpose(kv_all, (0, 1, 2, 4, 3, 5, 6)).reshape(2, kv_local, tokens, head_dim)
    key_rows = kv_all[0]
    value_rows = kv_all[1]

    chunk_rows = group_rows // Q_CHUNKS
    member_part = local_rows // Q_CHUNKS
    q_chunks = jnp.transpose(
        q_rot.reshape(n_group, Q_CHUNKS, member_part, n_pair, head_dim), (1, 0, 2, 3, 4)
    ).reshape(Q_CHUNKS, chunk_rows, kv_local, 2, head_dim)
    q_ids = jnp.transpose(row_ids.reshape(n_group, Q_CHUNKS, member_part), (1, 0, 2)).reshape(
        Q_CHUNKS, chunk_rows
    )
    q_segs = jnp.transpose(
        row_segments.reshape(n_group, Q_CHUNKS, member_part), (1, 0, 2)
    ).reshape(Q_CHUNKS, chunk_rows)
    q_pos = jnp.transpose(positions.reshape(n_group, Q_CHUNKS, member_part), (1, 0, 2)).reshape(
        Q_CHUNKS, chunk_rows
    )

    def attend(chunk):
        def tile(tile_index, state):
            numer_one, denom_one = state
            k_start = tile_index * KEY_TILE
            k_block = lax.dynamic_slice_in_dim(key_rows, k_start, KEY_TILE, 1)
            v_block = lax.dynamic_slice_in_dim(value_rows, k_start, KEY_TILE, 1)
            k_segs = lax.dynamic_slice_in_dim(segment_ids, k_start, KEY_TILE, 0)
            k_ids = k_start + jnp.arange(KEY_TILE, dtype=jnp.int32)

            scores = (
                jnp.einsum(
                    "qkgd,ktd->kgqt",
                    q_chunks[chunk],
                    k_block,
                    preferred_element_type=jnp.float32,
                )
                * QUERY_SCALE
            )
            scores = SOFTCAP * jnp.tanh(scores / SOFTCAP)
            live = (k_ids[None, :] <= q_ids[chunk][:, None]) & (
                k_segs[None, :] == q_segs[chunk][:, None]
            )
            weights = jnp.where(live[None, None], jnp.exp(scores - SCORE_SHIFT), 0.0)
            denom_one = denom_one + jnp.sum(weights, axis=-1)
            numer_one = numer_one + jnp.einsum(
                "kgqt,ktd->qkgd",
                weights.astype(jnp.bfloat16),
                v_block,
                preferred_element_type=jnp.float32,
            )
            return (numer_one, denom_one)

        zero_numer = jnp.zeros((chunk_rows, kv_local, 2, head_dim), jnp.float32)
        zero_denom = jnp.zeros((kv_local, 2, chunk_rows), jnp.float32)
        lo_tile = jnp.min(q_ids[chunk] - q_pos[chunk]) // KEY_TILE
        hi_tile = jnp.max(q_ids[chunk]) // KEY_TILE + 1
        numer, denom = lax.fori_loop(lo_tile, hi_tile, tile, (zero_numer, zero_denom))
        denom_rows = jnp.transpose(denom, (2, 0, 1))[..., None]
        attended = (numer / denom_rows).astype(jnp.bfloat16).reshape(
            chunk_rows, n_pair * head_dim
        )
        partial = jnp.dot(attended, pair_out, preferred_element_type=jnp.float32).astype(
            jnp.bfloat16
        )
        pieces = lax.all_to_all(
            partial.reshape(n_group, member_part, -1), "th", 0, 0, tiled=True
        )
        return jnp.sum(pieces.astype(jnp.float32), axis=0)

    projected = jnp.concatenate([attend(chunk) for chunk in range(Q_CHUNKS)], axis=0)
    hidden_out = (hidden + rms_scale(projected, post_gain)).astype(jnp.bfloat16)

    cache_len = tokens // 2
    part_len = cache_len // n_seq
    request_ids = jnp.arange(slot_count, dtype=jnp.int32)
    starts = jnp.cumsum(seg_lengths) - seg_lengths
    own_head = pair_index // 2
    own_offset = pair_index % 2 * half_kv
    own_keys = lax.dynamic_slice_in_dim(
        lax.dynamic_index_in_dim(key_rows, own_head, 0, keepdims=False), own_offset, half_kv, 1
    )
    own_values = lax.dynamic_slice_in_dim(
        lax.dynamic_index_in_dim(value_rows, own_head, 0, keepdims=False), own_offset, half_kv, 1
    )
    keys_pad = jnp.concatenate([own_keys, jnp.zeros((cache_len, half_kv), jnp.bfloat16)], 0)
    values_pad = jnp.concatenate(
        [own_values, jnp.zeros((cache_len, half_kv), jnp.bfloat16)], 0
    )
    seg_pad = jnp.concatenate([segment_ids, jnp.full((cache_len,), -1, jnp.int32)], 0)
    key_slots = []
    value_slots = []
    for slot_index in range(slot_count):
        request = jnp.sum(jnp.where(slot_map == slot_index, request_ids, 0)).astype(jnp.int32)
        first_row = jnp.sum(jnp.where(request_ids == request, starts, 0)).astype(jnp.int32)
        row0 = first_row + seq_index * part_len
        keep = (lax.dynamic_slice_in_dim(seg_pad, row0, part_len, 0) == request)[:, None]
        key_slots.append(
            jnp.where(
                keep,
                lax.dynamic_slice_in_dim(keys_pad, row0, part_len, 0),
                jnp.zeros((), jnp.bfloat16),
            )
        )
        value_slots.append(
            jnp.where(
                keep,
                lax.dynamic_slice_in_dim(values_pad, row0, part_len, 0),
                jnp.zeros((), jnp.bfloat16),
            )
        )
    return (hidden_out, jnp.stack(key_slots), jnp.stack(value_slots))


def solution(mesh):
    devices = np.asarray(mesh.devices)
    n_seq, n_tensor = devices.shape
    split = Mesh(
        devices.reshape(n_seq, n_tensor // HEADS_PER_DEVICE, HEADS_PER_DEVICE),
        ("seq", "th", "tl"),
    )
    rows = P(("seq", "th", "tl"), None)
    cols = P(None, ("th", "tl"))
    return jax.shard_map(
        on_device,
        mesh=split,
        in_specs=(
            rows,
            P(),
            cols,
            cols,
            cols,
            P(("th", "tl"), None),
            P(),
            P(),
            P(),
            P(),
        ),
        out_specs=(rows, P(None, "seq", ("th", "tl")), P(None, "seq", ("th", "tl"))),
        check_vma=False,
    )
```
